128 devices in a mesh: dp: 32 (over y, x, core), blk: 4 (over z).
Axes of the slice: x: 4, y: 4, z: 4, core: 2. Of those that a mesh axis runs over, the one named last changes fastest.
Arguments:
- prod_feat: bfloat16 [32, 3072, 768], P('dp', 'blk'), may hold values from -23 to 23
- prec_feat: bfloat16 [32, 3072, 768], P('dp', 'blk'), may hold values from -23 to 23
- matched: int32 [32, 3072], P('dp', 'blk'), may hold values from 0 to 3071, each once within a row
- row_weight: float32 [32, 3072], P('dp', 'blk'), may hold values from 0.2 to 28, as said below
- proj_prod: bfloat16 [768, 1024], replicated, may hold values from -0.21875 to 0.21875
- proj_prec: bfloat16 [768, 1024], replicated, may hold values from -0.21875 to 0.21875
Outputs:
- loss_value: float32 [], replicated
- grad_prod: float32 [768, 1024], P('dp', 'blk')
- grad_prec: float32 [768, 1024], P('dp', 'blk')
The draws below stay inside these ranges and needn't reach their ends.
Inputs may be any that keep to these rules, and one draw needn't show every extreme that they name: `matched`: in each of the 32 groups the 3072 values are a permutation of 0 to 3071. `row_weight`: positive.
All inputs are finite; a program needn't handle non-finite values.
Results may differ from the reference program's by a relative error of at most 0.0027.
Values may be sent and summed in bfloat16 or wider, within the bound.
No kernel may reach another device: no remote copies, remote signals or barrier semaphores. Data moves between devices by JAX's collectives and lax.ppermute only.
A program may use at most 128 MiB of HBM per device.

```python
import jax
import jax.numpy as jnp
from jax import lax

FEAT = 768
EMBED = 1024
GROUP = 3072
N_DP = 32


def feature_draw(key):
    col_key, val_key = jax.random.split(key, 2)
    exponent = jax.random.uniform(col_key, (FEAT,), jnp.float32, 0.0, 1.5)
    scales = 10.0 ** (exponent - 0.75)
    values = jax.random.truncated_normal(val_key, -4.0, 4.0, (N_DP, GROUP, FEAT), jnp.float32)
    return (values * scales).astype(jnp.bfloat16)


def draw_prod_feat(key, part):
    return feature_draw(jax.random.fold_in(key, 11))


def draw_prec_feat(key, part):
    return feature_draw(jax.random.fold_in(key, 23))


def draw_row_weight(key, part):
    base_key = jax.random.fold_in(key, 37)
    base = jnp.exp(jax.random.uniform(base_key, (N_DP, GROUP), jnp.float32, -1.2, 1.1))
    group_frac = jnp.arange(N_DP, dtype=jnp.float32) / max(N_DP - 1, 1)
    row_frac = jnp.arange(GROUP, dtype=jnp.float32) / max(GROUP - 1, 1)
    ramp = (3.0 ** group_frac)[:, None] * (3.0 ** row_frac)[None, :]
    return base * ramp


def bell_draw(stream_key, dims, deviation, limit, held_as=jnp.bfloat16):
    return jnp.clip(deviation * jax.random.normal(stream_key, dims, jnp.float32), -limit, limit).astype(held_as)


def setup_inputs(seed: int = 0) -> dict:
    splits = jax.random.split(jax.random.key(seed), 7)
    prod_feat = draw_prod_feat(jax.random.fold_in(splits[6], 71), 0)
    prec_feat = draw_prec_feat(jax.random.fold_in(splits[6], 71), 0)
    matched = jax.vmap(lambda own: jax.random.permutation(own, GROUP))(jax.random.split(splits[2], N_DP)).reshape((N_DP, GROUP)).astype(jnp.int32)
    row_weight = draw_row_weight(jax.random.fold_in(splits[6], 71), 0)
    proj_prod = bell_draw(splits[4], (FEAT, EMBED), FEAT ** -0.5, 0.21875)
    proj_prec = bell_draw(splits[5], (FEAT, EMBED), FEAT ** -0.5, 0.21875)
    return dict(prod_feat=prod_feat, prec_feat=prec_feat, matched=matched, row_weight=row_weight, proj_prod=proj_prod, proj_prec=proj_prec)


EPS = 1e-06
LOGIT_SCALE = 50.0

def embed_rows(features, weight):
    projected_raw = jnp.dot(features, weight, preferred_element_type=jnp.float32)
    radius = jnp.sqrt(lax.optimization_barrier(jnp.sum(projected_raw * projected_raw, axis=1, keepdims=True)) + EPS)
    unit_vec = projected_raw / radius
    return (unit_vec, unit_vec.astype(jnp.bfloat16), radius)

def similarity(queries, key_rows):
    return LOGIT_SCALE * lax.dot_general(queries, key_rows, (((1,), (1,)), ((), ())), preferred_element_type=jnp.float32)

def coefficient(scores, matches, weights, totals):
    probability = jnp.exp(scores - LOGIT_SCALE) / totals[:, None]
    return (weights[:, None] * (probability - matches.astype(jnp.float32))).astype(jnp.bfloat16)

def back_norm(unit_vec, radius, gradient):
    projected = lax.optimization_barrier(jnp.sum(unit_vec * gradient, axis=1, keepdims=True))
    return ((gradient - unit_vec * projected) / radius).astype(jnp.bfloat16)

def reference(prod_feat, prec_feat, matched, row_weight, proj_prod, proj_prec):

    def one_group(inputs):
        feat_prod, feat_prec, targets, weights = inputs
        unit_prod, unit16_prod, radius_prod = embed_rows(feat_prod, proj_prod)
        unit_prec, unit16_prec, radius_prec = embed_rows(feat_prec, proj_prec)
        scores = similarity(unit16_prod, unit16_prec)
        columns = jnp.arange(GROUP, dtype=jnp.int32)
        matches = targets[:, None] == columns[None, :]
        totals = lax.optimization_barrier(jnp.sum(jnp.exp(scores - LOGIT_SCALE), axis=1))
        positive = lax.optimization_barrier(jnp.sum(jnp.where(matches, scores, 0.0), axis=1))
        losses = LOGIT_SCALE + jnp.log(totals) - positive
        coeffs = coefficient(scores, matches, weights, totals)
        grad_unit_prod = LOGIT_SCALE * jnp.dot(coeffs, unit16_prec, preferred_element_type=jnp.float32)
        grad_unit_prec = LOGIT_SCALE * lax.dot_general(coeffs, unit16_prod, (((0,), (0,)), ((), ())), preferred_element_type=jnp.float32)
        dir_prod = back_norm(unit_prod, radius_prod, grad_unit_prod)
        dir_prec = back_norm(unit_prec, radius_prec, grad_unit_prec)
        head_prod = lax.dot_general(feat_prod, dir_prod, (((0,), (0,)), ((), ())), preferred_element_type=jnp.float32)
        head_prec = lax.dot_general(feat_prec, dir_prec, (((0,), (0,)), ((), ())), preferred_element_type=jnp.float32)
        return (jnp.sum(weights * losses), jnp.sum(weights), head_prod, head_prec)
    loss_sums, weight_sums, heads_prod, heads_prec = lax.map(one_group, (prod_feat, prec_feat, matched, row_weight))
    weight_total = jnp.sum(weight_sums)
    return (jnp.sum(loss_sums) / weight_total, lax.optimization_barrier(jnp.sum(heads_prod, axis=0)) / weight_total, lax.optimization_barrier(jnp.sum(heads_prec, axis=0)) / weight_total)
```

```python
import jax
import jax.numpy as jnp
from jax import lax
from jax.sharding import PartitionSpec as P

EPS = 1e-06
LOGIT_SCALE = 50.0


def embed_rows(features, weight):
    projected_raw = jnp.dot(features, weight, preferred_element_type=jnp.float32)
    radius = jnp.sqrt(jnp.sum(projected_raw * projected_raw, axis=1, keepdims=True) + EPS)
    unit_vec = projected_raw / radius
    return (unit_vec, unit_vec.astype(jnp.bfloat16), radius)


def similarity(queries, key_rows):
    return LOGIT_SCALE * lax.dot_general(
        queries, key_rows, (((1,), (1,)), ((), ())), preferred_element_type=jnp.float32
    )


def coefficient(scores, matches, weights, totals):
    probability = jnp.exp(scores - LOGIT_SCALE) / totals[:, None]
    return (weights[:, None] * (probability - matches.astype(jnp.float32))).astype(jnp.bfloat16)


def back_norm(unit_vec, radius, gradient):
    projected = jnp.sum(unit_vec * gradient, axis=1, keepdims=True)
    return ((gradient - unit_vec * projected) / radius).astype(jnp.bfloat16)


def spread_blocks(head, dp_size, blk_size):
    feat, embed = head.shape
    tiles = head.reshape(dp_size, feat // dp_size, blk_size, embed // blk_size)
    tiles = tiles.transpose(0, 2, 1, 3)
    return tiles.reshape(dp_size * blk_size * (feat // dp_size), embed // blk_size)


def per_device(prod_feat, prec_feat, matched, row_weight, proj_prod, proj_prec):
    feat_prod = prod_feat[0]
    feat_prec = prec_feat[0]
    targets = matched[0]
    weights = row_weight[0]
    dp_size = lax.axis_size("dp")
    blk_size = lax.axis_size("blk")
    unit_prod, unit16_prod, radius_prod = embed_rows(feat_prod, proj_prod)
    feat_prec_all = lax.all_gather(feat_prec, "blk", axis=0, tiled=True)
    unit_prec, unit16_prec, radius_prec = embed_rows(feat_prec_all, proj_prec)
    scores = similarity(unit16_prod, unit16_prec)
    columns = lax.iota(jnp.int32, unit16_prec.shape[0])
    matches = targets[:, None] == columns[None, :]
    totals = jnp.sum(jnp.exp(scores - LOGIT_SCALE), axis=1)
    positive = jnp.sum(jnp.where(matches, scores, 0.0), axis=1)
    losses = LOGIT_SCALE + jnp.log(totals) - positive
    loss_local = jnp.sum(weights * losses)
    weight_local = jnp.sum(weights)
    loss_sum, weight_total = lax.psum((loss_local, weight_local), ("dp", "blk"))
    coeffs = coefficient(scores, matches, weights, totals)
    grad_unit_prod = LOGIT_SCALE * jnp.dot(coeffs, unit16_prec, preferred_element_type=jnp.float32)
    grad_prec_part = LOGIT_SCALE * lax.dot_general(
        coeffs, unit16_prod, (((0,), (0,)), ((), ())), preferred_element_type=jnp.float32
    )
    dir_prod = back_norm(unit_prod, radius_prod, grad_unit_prod)
    dir_prec = back_norm(unit_prec, radius_prec, grad_prec_part)
    head_prod = lax.dot_general(
        feat_prod, dir_prod, (((0,), (0,)), ((), ())), preferred_element_type=jnp.float32
    )
    head_prec = lax.dot_general(
        feat_prec_all, dir_prec, (((0,), (0,)), ((), ())), preferred_element_type=jnp.float32
    )
    summed_prod = lax.psum_scatter(
        spread_blocks(head_prod, dp_size, blk_size), ("dp", "blk"), scatter_dimension=0, tiled=True
    )
    summed_prec = lax.psum_scatter(
        spread_blocks(head_prec, dp_size, blk_size), ("dp", "blk"), scatter_dimension=0, tiled=True
    )
    return (loss_sum / weight_total, summed_prod / weight_total, summed_prec / weight_total)


def solution(mesh):
    placed = (P("dp", "blk", None), P("dp", "blk", None), P("dp", "blk"), P("dp", "blk"), P(), P())
    return jax.shard_map(
        per_device,
        mesh=mesh,
        in_specs=placed,
        out_specs=(P(), P("dp", "blk"), P("dp", "blk")),
        check_vma=False,
    )
```

```python
import jax
import jax.numpy as jnp
from jax import lax
from jax.sharding import Mesh, PartitionSpec as P

EPS = 1e-06
LOGIT_SCALE = 50.0


def embed_rows(features, weight):
    projected_raw = jnp.dot(features, weight, preferred_element_type=jnp.float32)
    radius = jnp.sqrt(jnp.sum(projected_raw * projected_raw, axis=1, keepdims=True) + EPS)
    unit_vec = projected_raw / radius
    return (unit_vec, unit_vec.astype(jnp.bfloat16), radius)


def similarity(queries, key_rows):
    return LOGIT_SCALE * lax.dot_general(
        queries, key_rows, (((1,), (1,)), ((), ())), preferred_element_type=jnp.float32
    )


def coefficient(scores, matches, weights, totals):
    probability = jnp.exp(scores - LOGIT_SCALE) / totals[:, None]
    return (weights[:, None] * (probability - matches.astype(jnp.float32))).astype(jnp.bfloat16)


def back_norm(unit_vec, radius, gradient):
    projected = jnp.sum(unit_vec * gradient, axis=1, keepdims=True)
    return ((gradient - unit_vec * projected) / radius).astype(jnp.bfloat16)


def per_device(prod_feat, prec_feat, matched, row_weight, proj_prod, proj_prec):
    feat_prod = prod_feat[0]
    feat_prec = prec_feat[0]
    targets = matched[0]
    weights = row_weight[0]
    unit_prod, unit16_prod, radius_prod = embed_rows(feat_prod, proj_prod)
    feat_prec_all = lax.all_gather(feat_prec, "blk", axis=0, tiled=True)
    unit_prec, unit16_prec, radius_prec = embed_rows(feat_prec_all, proj_prec)
    scores = similarity(unit16_prod, unit16_prec)
    columns = lax.iota(jnp.int32, unit16_prec.shape[0])
    matches = targets[:, None] == columns[None, :]
    totals = jnp.sum(jnp.exp(scores - LOGIT_SCALE), axis=1)
    positive = jnp.sum(jnp.where(matches, scores, 0.0), axis=1)
    losses = LOGIT_SCALE + jnp.log(totals) - positive
    loss_local = jnp.sum(weights * losses)
    weight_local = jnp.sum(weights)
    scalars = lax.psum(jnp.stack([loss_local, weight_local]), ("y", "x", "core", "blk"))
    loss_sum = scalars[0]
    weight_total = scalars[1]
    coeffs = coefficient(scores, matches, weights, totals)
    grad_unit_prod = LOGIT_SCALE * jnp.dot(coeffs, unit16_prec, preferred_element_type=jnp.float32)
    grad_prec_part = LOGIT_SCALE * lax.dot_general(
        coeffs, unit16_prod, (((0,), (0,)), ((), ())), preferred_element_type=jnp.float32
    )
    dir_prod = back_norm(unit_prod, radius_prod, grad_unit_prod)
    dir_prec = back_norm(unit_prec, radius_prec, grad_prec_part)
    head_prod = lax.dot_general(
        feat_prod, dir_prod, (((0,), (0,)), ((), ())), preferred_element_type=jnp.float32
    )
    head_prec = lax.dot_general(
        feat_prec_all, dir_prec, (((0,), (0,)), ((), ())), preferred_element_type=jnp.float32
    )
    heads = jnp.stack([head_prod, head_prec])
    feat, embed = head_prod.shape
    y_size = lax.axis_size("y")
    x_size = lax.axis_size("x")
    core_size = lax.axis_size("core")
    heads = heads.reshape(2, y_size, x_size, core_size, feat // (y_size * x_size * core_size), embed)
    heads = lax.psum_scatter(heads, "core", scatter_dimension=3, tiled=False)
    heads = lax.psum_scatter(heads, "x", scatter_dimension=2, tiled=False)
    heads = lax.psum_scatter(heads, "y", scatter_dimension=1, tiled=False)
    heads = lax.psum_scatter(heads, "blk", scatter_dimension=2, tiled=True)
    heads = heads / weight_total
    return (loss_sum / weight_total, heads[0], heads[1])


def solution(mesh):
    dp_size = mesh.shape["dp"]
    blk_size = mesh.shape["blk"]
    lanes = mesh.devices.reshape(dp_size // 8, 4, 2, blk_size)
    fine = Mesh(lanes, ("y", "x", "core", "blk"))
    rows = ("y", "x", "core")
    placed = (P(rows, "blk", None), P(rows, "blk", None), P(rows, "blk"), P(rows, "blk"), P(), P())
    return jax.shard_map(
        per_device,
        mesh=fine,
        in_specs=placed,
        out_specs=(P(), P(rows, "blk"), P(rows, "blk")),
        check_vma=False,
    )
```

```python
import jax
import jax.numpy as jnp
from jax import lax
from jax.sharding import Mesh, PartitionSpec as P

EPS = 1e-06
LOGIT_SCALE = 50.0


def embed_rows(features, weight):
    projected_raw = jnp.dot(features, weight, preferred_element_type=jnp.float32)
    radius = jnp.sqrt(jnp.sum(projected_raw * projected_raw, axis=1, keepdims=True) + EPS)
    unit_vec = projected_raw / radius
    return (unit_vec, unit_vec.astype(jnp.bfloat16), radius)


def similarity(queries, key_rows):
    return LOGIT_SCALE * lax.dot_general(
        queries, key_rows, (((1,), (1,)), ((), ())), preferred_element_type=jnp.float32
    )


def coefficient(scores, matches, weights, totals):
    probability = jnp.exp(scores - LOGIT_SCALE) / totals[:, None]
    return (weights[:, None] * (probability - matches.astype(jnp.float32))).astype(jnp.bfloat16)


def back_norm(unit_vec, radius, gradient):
    projected = jnp.sum(unit_vec * gradient, axis=1, keepdims=True)
    return ((gradient - unit_vec * projected) / radius).astype(jnp.bfloat16)


def gather_along(values, axis):
    size = lax.axis_size(axis)
    pieces = [values]
    for shift in range(1, size):
        route = [(i, (i + shift) % size) for i in range(size)]
        pieces.append(lax.ppermute(values, axis, route))
    stacked = jnp.stack(pieces)
    order = (lax.axis_index(axis) - jnp.arange(size)) % size
    return stacked[order]


def per_device(prod_feat, prec_feat, matched, row_weight, proj_prod, proj_prec):
    feat_prod = prod_feat[0]
    feat_prec = prec_feat[0]
    targets = matched[0]
    weights = row_weight[0]
    unit_prod, unit16_prod, radius_prod = embed_rows(feat_prod, proj_prod)
    feat_prec_all = lax.all_gather(feat_prec, "blk", axis=0, tiled=True)
    unit_prec, unit16_prec, radius_prec = embed_rows(feat_prec_all, proj_prec)
    scores = similarity(unit16_prod, unit16_prec)
    columns = lax.iota(jnp.int32, unit16_prec.shape[0])
    matches = targets[:, None] == columns[None, :]
    totals = jnp.sum(jnp.exp(scores - LOGIT_SCALE), axis=1)
    positive = jnp.sum(jnp.where(matches, scores, 0.0), axis=1)
    losses = LOGIT_SCALE + jnp.log(totals) - positive
    loss_local = jnp.sum(weights * losses)
    weight_local = jnp.sum(weights)
    scalars = jnp.stack([loss_local, weight_local])
    for axis in ("core", "x", "y", "blk"):
        scalars = gather_along(scalars, axis)
    scalars = scalars.reshape(-1, 2)
    loss_sum = jnp.sum(scalars[:, 0])
    weight_total = jnp.sum(scalars[:, 1])
    coeffs = coefficient(scores, matches, weights, totals)
    grad_unit_prod = LOGIT_SCALE * jnp.dot(coeffs, unit16_prec, preferred_element_type=jnp.float32)
    grad_prec_part = LOGIT_SCALE * lax.dot_general(
        coeffs, unit16_prod, (((0,), (0,)), ((), ())), preferred_element_type=jnp.float32
    )
    dir_prod = back_norm(unit_prod, radius_prod, grad_unit_prod)
    dir_prec = back_norm(unit_prec, radius_prec, grad_prec_part)
    head_prod = lax.dot_general(
        feat_prod, dir_prod, (((0,), (0,)), ((), ())), preferred_element_type=jnp.float32
    )
    head_prec = lax.dot_general(
        feat_prec_all, dir_prec, (((0,), (0,)), ((), ())), preferred_element_type=jnp.float32
    )
    heads = jnp.stack([head_prod, head_prec])
    feat, embed = head_prod.shape
    y_size = lax.axis_size("y")
    x_size = lax.axis_size("x")
    core_size = lax.axis_size("core")
    heads = heads.reshape(2, y_size, x_size, core_size, feat // (y_size * x_size * core_size), embed)
    heads = lax.psum_scatter(heads, "core", scatter_dimension=3, tiled=False)
    heads = lax.psum_scatter(heads, "x", scatter_dimension=2, tiled=False)
    heads = lax.psum_scatter(heads, "y", scatter_dimension=1, tiled=False)
    heads = lax.psum_scatter(heads, "blk", scatter_dimension=2, tiled=True)
    heads = heads / weight_total
    return (loss_sum / weight_total, heads[0], heads[1])


def solution(mesh):
    dp_size = mesh.shape["dp"]
    blk_size = mesh.shape["blk"]
    lanes = mesh.devices.reshape(dp_size // 8, 4, 2, blk_size)
    fine = Mesh(lanes, ("y", "x", "core", "blk"))
    rows = ("y", "x", "core")
    placed = (P(rows, "blk", None), P(rows, "blk", None), P(rows, "blk"), P(rows, "blk"), P(), P())
    return jax.shard_map(
        per_device,
        mesh=fine,
        in_specs=placed,
        out_specs=(P(), P(rows, "blk"), P(rows, "blk")),
        check_vma=False,
    )
```

```python
import jax
import jax.numpy as jnp
from jax import lax
from jax.sharding import Mesh, PartitionSpec as P

EPS = 1e-06
LOGIT_SCALE = 50.0


def embed_rows(features, weight):
    projected_raw = jnp.dot(features, weight, preferred_element_type=jnp.float32)
    radius = jnp.sqrt(jnp.sum(projected_raw * projected_raw, axis=1, keepdims=True) + EPS)
    unit_vec = projected_raw / radius
    return (unit_vec, unit_vec.astype(jnp.bfloat16), radius)


def similarity(queries, key_rows):
    return LOGIT_SCALE * lax.dot_general(
        queries, key_rows, (((1,), (1,)), ((), ())), preferred_element_type=jnp.float32
    )


def coefficient(scores, matches, weights, totals):
    probability = jnp.exp(scores - LOGIT_SCALE) / totals[:, None]
    return (weights[:, None] * (probability - matches.astype(jnp.float32))).astype(jnp.bfloat16)


def back_norm(unit_vec, radius, gradient):
    projected = jnp.sum(unit_vec * gradient, axis=1, keepdims=True)
    return ((gradient - unit_vec * projected) / radius).astype(jnp.bfloat16)


def gather_along(values, axis):
    size = lax.axis_size(axis)
    pieces = [values]
    for shift in range(1, size):
        route = [(i, (i + shift) % size) for i in range(size)]
        pieces.append(lax.ppermute(values, axis, route))
    stacked = jnp.stack(pieces)
    order = (lax.axis_index(axis) - jnp.arange(size)) % size
    return stacked[order]


def scatter_sum(values, axis, dim):
    size = lax.axis_size(axis)
    own = lax.axis_index(axis)
    total = lax.dynamic_index_in_dim(values, own, axis=dim, keepdims=False)
    for shift in range(1, size):
        route = [(i, (i + shift) % size) for i in range(size)]
        piece = lax.dynamic_index_in_dim(values, (own + shift) % size, axis=dim, keepdims=False)
        total = total + lax.ppermute(piece, axis, route)
    return total


def per_device(prod_feat, prec_feat, matched, row_weight, proj_prod, proj_prec):
    feat_prod = prod_feat[0]
    feat_prec = prec_feat[0]
    targets = matched[0]
    weights = row_weight[0]
    unit_prod, unit16_prod, radius_prod = embed_rows(feat_prod, proj_prod)
    feat_prec_all = lax.all_gather(feat_prec, "blk", axis=0, tiled=True)
    unit_prec, unit16_prec, radius_prec = embed_rows(feat_prec_all, proj_prec)
    scores = similarity(unit16_prod, unit16_prec)
    columns = lax.iota(jnp.int32, unit16_prec.shape[0])
    matches = targets[:, None] == columns[None, :]
    totals = jnp.sum(jnp.exp(scores - LOGIT_SCALE), axis=1)
    positive = jnp.sum(jnp.where(matches, scores, 0.0), axis=1)
    losses = LOGIT_SCALE + jnp.log(totals) - positive
    loss_local = jnp.sum(weights * losses)
    weight_local = jnp.sum(weights)
    scalars = jnp.stack([loss_local, weight_local])
    for axis in ("core", "x", "y", "blk"):
        scalars = gather_along(scalars, axis)
    scalars = scalars.reshape(-1, 2)
    loss_sum = jnp.sum(scalars[:, 0])
    weight_total = jnp.sum(scalars[:, 1])
    coeffs = coefficient(scores, matches, weights, totals)
    grad_unit_prod = LOGIT_SCALE * jnp.dot(coeffs, unit16_prec, preferred_element_type=jnp.float32)
    grad_prec_part = LOGIT_SCALE * lax.dot_general(
        coeffs, unit16_prod, (((0,), (0,)), ((), ())), preferred_element_type=jnp.float32
    )
    dir_prod = back_norm(unit_prod, radius_prod, grad_unit_prod)
    dir_prec = back_norm(unit_prec, radius_prec, grad_prec_part)
    head_prod = lax.dot_general(
        feat_prod, dir_prod, (((0,), (0,)), ((), ())), preferred_element_type=jnp.float32
    )
    head_prec = lax.dot_general(
        feat_prec_all, dir_prec, (((0,), (0,)), ((), ())), preferred_element_type=jnp.float32
    )
    heads = jnp.stack([head_prod, head_prec])
    feat, embed = head_prod.shape
    y_size = lax.axis_size("y")
    x_size = lax.axis_size("x")
    core_size = lax.axis_size("core")
    blk_size = lax.axis_size("blk")
    block_rows = feat // (y_size * x_size * core_size)
    heads = heads.reshape(
        2, y_size, x_size, core_size, 3, block_rows // 3, blk_size, embed // blk_size
    )
    heads = scatter_sum(heads, "core", 3)
    first = scatter_sum(heads[:, :, :, 0], "x", 2)
    first = scatter_sum(first, "y", 1)
    first = scatter_sum(first, "blk", 2)
    second = scatter_sum(heads[:, :, :, 1], "y", 1)
    second = scatter_sum(second, "blk", 3)
    second = scatter_sum(second, "x", 1)
    third = scatter_sum(heads[:, :, :, 2], "blk", 4)
    third = scatter_sum(third, "x", 2)
    third = scatter_sum(third, "y", 1)
    heads = jnp.concatenate([first, second, third], axis=1)
    heads = heads / weight_total
    return (loss_sum / weight_total, heads[0], heads[1])


def solution(mesh):
    dp_size = mesh.shape["dp"]
    blk_size = mesh.shape["blk"]
    lanes = mesh.devices.reshape(dp_size // 8, 4, 2, blk_size)
    fine = Mesh(lanes, ("y", "x", "core", "blk"))
    rows = ("y", "x", "core")
    placed = (P(rows, "blk", None), P(rows, "blk", None), P(rows, "blk"), P(rows, "blk"), P(), P())
    return jax.shard_map(
        per_device,
        mesh=fine,
        in_specs=placed,
        out_specs=(P(), P(rows, "blk"), P(rows, "blk")),
        check_vma=False,
    )
```

```python
import jax
import jax.numpy as jnp
from jax import lax
from jax.sharding import Mesh, PartitionSpec as P

EPS = 1e-06
LOGIT_SCALE = 50.0


def embed_rows(features, weight):
    projected_raw = jnp.dot(features, weight, preferred_element_type=jnp.float32)
    radius = jnp.sqrt(jnp.sum(projected_raw * projected_raw, axis=1, keepdims=True) + EPS)
    unit_vec = projected_raw / radius
    return (unit_vec, unit_vec.astype(jnp.bfloat16), radius)


def similarity(queries, key_rows):
    return LOGIT_SCALE * lax.dot_general(
        queries, key_rows, (((1,), (1,)), ((), ())), preferred_element_type=jnp.float32
    )


def coefficient(scores, matches, weights, totals):
    probability = jnp.exp(scores - LOGIT_SCALE) / totals[:, None]
    return (weights[:, None] * (probability - matches.astype(jnp.float32))).astype(jnp.bfloat16)


def back_norm(unit_vec, radius, gradient):
    projected = jnp.sum(unit_vec * gradient, axis=1, keepdims=True)
    return ((gradient - unit_vec * projected) / radius).astype(jnp.bfloat16)


def gather_along(values, axis):
    size = lax.axis_size(axis)
    pieces = [values]
    for shift in range(1, size):
        route = [(i, (i + shift) % size) for i in range(size)]
        pieces.append(lax.ppermute(values, axis, route))
    stacked = jnp.stack(pieces)
    order = (lax.axis_index(axis) - jnp.arange(size)) % size
    return stacked[order]


def scatter_sum(values, axis, dim):
    size = lax.axis_size(axis)
    own = lax.axis_index(axis)
    total = lax.dynamic_index_in_dim(values, own, axis=dim, keepdims=False)
    for shift in range(1, size):
        route = [(i, (i + shift) % size) for i in range(size)]
        piece = lax.dynamic_index_in_dim(values, (own + shift) % size, axis=dim, keepdims=False)
        total = total + lax.ppermute(piece, axis, route)
    return total


def per_device(prod_feat, prec_feat, matched, row_weight, proj_prod, proj_prec):
    feat_prod = prod_feat[0]
    feat_prec = prec_feat[0]
    targets = matched[0]
    weights = row_weight[0]
    unit_prod, unit16_prod, radius_prod = embed_rows(feat_prod, proj_prod)
    feat_prec_all = lax.all_gather(feat_prec, "blk", axis=0, tiled=True)
    unit_prec, unit16_prec, radius_prec = embed_rows(feat_prec_all, proj_prec)
    scores = similarity(unit16_prod, unit16_prec)
    columns = lax.iota(jnp.int32, unit16_prec.shape[0])
    matches = targets[:, None] == columns[None, :]
    totals = jnp.sum(jnp.exp(scores - LOGIT_SCALE), axis=1)
    positive = jnp.sum(jnp.where(matches, scores, 0.0), axis=1)
    losses = LOGIT_SCALE + jnp.log(totals) - positive
    loss_local = jnp.sum(weights * losses)
    weight_local = jnp.sum(weights)
    scalars = jnp.stack([loss_local, weight_local])
    for axis in ("core", "x", "y", "blk"):
        scalars = gather_along(scalars, axis)
    scalars = scalars.reshape(-1, 2)
    loss_sum = jnp.sum(scalars[:, 0])
    weight_total = jnp.sum(scalars[:, 1])
    coeffs = coefficient(scores, matches, weights, totals)
    grad_unit_prod = LOGIT_SCALE * jnp.dot(coeffs, unit16_prec, preferred_element_type=jnp.float32)
    grad_prec_part = LOGIT_SCALE * lax.dot_general(
        coeffs, unit16_prod, (((0,), (0,)), ((), ())), preferred_element_type=jnp.float32
    )
    dir_prod = back_norm(unit_prod, radius_prod, grad_unit_prod)
    dir_prec = back_norm(unit_prec, radius_prec, grad_prec_part)
    head_prod = lax.dot_general(
        feat_prod, dir_prod, (((0,), (0,)), ((), ())), preferred_element_type=jnp.float32
    )
    head_prec = lax.dot_general(
        feat_prec_all, dir_prec, (((0,), (0,)), ((), ())), preferred_element_type=jnp.float32
    )
    heads = jnp.stack([head_prod, head_prec])
    feat, embed = head_prod.shape
    y_size = lax.axis_size("y")
    x_size = lax.axis_size("x")
    core_size = lax.axis_size("core")
    blk_size = lax.axis_size("blk")
    block_rows = feat // (y_size * x_size * core_size)
    heads = heads.reshape(2, y_size, x_size, core_size, block_rows, blk_size, embed // blk_size)
    heads = heads.transpose(3, 2, 1, 5, 0, 4, 6)
    heads = lax.psum_scatter(heads, "core", scatter_dimension=0, tiled=False)
    heads = lax.psum_scatter(heads, "x", scatter_dimension=0, tiled=False)
    heads = scatter_sum(heads, "y", 0)
    heads = scatter_sum(heads, "blk", 0)
    heads = heads / weight_total
    return (loss_sum / weight_total, heads[0], heads[1])


def solution(mesh):
    dp_size = mesh.shape["dp"]
    blk_size = mesh.shape["blk"]
    lanes = mesh.devices.reshape(dp_size // 8, 4, 2, blk_size)
    fine = Mesh(lanes, ("y", "x", "core", "blk"))
    rows = ("y", "x", "core")
    placed = (P(rows, "blk", None), P(rows, "blk", None), P(rows, "blk"), P(rows, "blk"), P(), P())
    return jax.shard_map(
        per_device,
        mesh=fine,
        in_specs=placed,
        out_specs=(P(), P(rows, "blk"), P(rows, "blk")),
        check_vma=False,
    )
```

```python
import jax
import jax.numpy as jnp
from jax import lax
from jax.sharding import Mesh, PartitionSpec as P

EPS = 1e-06
LOGIT_SCALE = 50.0


def embed_rows(features, weight):
    projected_raw = jnp.dot(features, weight, preferred_element_type=jnp.float32)
    radius = jnp.sqrt(jnp.sum(projected_raw * projected_raw, axis=1, keepdims=True) + EPS)
    unit_vec = projected_raw / radius
    return (unit_vec, unit_vec.astype(jnp.bfloat16), radius)


def similarity(queries, key_rows):
    return LOGIT_SCALE * lax.dot_general(
        queries, key_rows, (((1,), (1,)), ((), ())), preferred_element_type=jnp.float32
    )


def coefficient(scores, matches, weights, totals):
    probability = jnp.exp(scores - LOGIT_SCALE) / totals[:, None]
    return (weights[:, None] * (probability - matches.astype(jnp.float32))).astype(jnp.bfloat16)


def back_norm(unit_vec, radius, gradient):
    projected = jnp.sum(unit_vec * gradient, axis=1, keepdims=True)
    return ((gradient - unit_vec * projected) / radius).astype(jnp.bfloat16)


def gather_along(values, axis):
    size = lax.axis_size(axis)
    pieces = [values]
    for shift in range(1, size):
        route = [(i, (i + shift) % size) for i in range(size)]
        pieces.append(lax.ppermute(values, axis, route))
    stacked = jnp.stack(pieces)
    order = (lax.axis_index(axis) - jnp.arange(size)) % size
    return stacked[order]


def per_device(prod_feat, prec_feat, matched, row_weight, proj_prod, proj_prec):
    feat_prod = prod_feat[0]
    feat_prec = prec_feat[0]
    targets = matched[0]
    weights = row_weight[0]
    unit_prod, unit16_prod, radius_prod = embed_rows(feat_prod, proj_prod)
    feat_prec_all = lax.all_gather(feat_prec, "blk", axis=0, tiled=True)
    unit_prec, unit16_prec, radius_prec = embed_rows(feat_prec_all, proj_prec)
    scores = similarity(unit16_prod, unit16_prec)
    columns = lax.iota(jnp.int32, unit16_prec.shape[0])
    matches = targets[:, None] == columns[None, :]
    totals = jnp.sum(jnp.exp(scores - LOGIT_SCALE), axis=1)
    positive = jnp.sum(jnp.where(matches, scores, 0.0), axis=1)
    losses = LOGIT_SCALE + jnp.log(totals) - positive
    loss_local = jnp.sum(weights * losses)
    weight_local = jnp.sum(weights)
    scalars = jnp.stack([loss_local, weight_local])
    for axis in ("core", "x", "y", "blk"):
        scalars = gather_along(scalars, axis)
    scalars = scalars.reshape(-1, 2)
    loss_sum = jnp.sum(scalars[:, 0])
    weight_total = jnp.sum(scalars[:, 1])
    coeffs = coefficient(scores, matches, weights, totals)
    grad_unit_prod = LOGIT_SCALE * jnp.dot(coeffs, unit16_prec, preferred_element_type=jnp.float32)
    grad_prec_part = LOGIT_SCALE * lax.dot_general(
        coeffs, unit16_prod, (((0,), (0,)), ((), ())), preferred_element_type=jnp.float32
    )
    dir_prod = back_norm(unit_prod, radius_prod, grad_unit_prod)
    dir_prec = back_norm(unit_prec, radius_prec, grad_prec_part)
    head_prod = lax.dot_general(
        feat_prod, dir_prod, (((0,), (0,)), ((), ())), preferred_element_type=jnp.float32
    )
    head_prec = lax.dot_general(
        feat_prec_all, dir_prec, (((0,), (0,)), ((), ())), preferred_element_type=jnp.float32
    )
    heads = jnp.stack([head_prod, head_prec])
    feat, embed = head_prod.shape
    y_size = lax.axis_size("y")
    x_size = lax.axis_size("x")
    core_size = lax.axis_size("core")
    heads = heads.reshape(2, y_size, x_size, core_size, feat // (y_size * x_size * core_size), embed)
    heads = lax.psum_scatter(heads, "core", scatter_dimension=3, tiled=False)
    heads = lax.psum_scatter(heads, "x", scatter_dimension=2, tiled=False)
    blk_size = lax.axis_size("blk")
    heads = heads.reshape(2, y_size, feat // (y_size * x_size * core_size), blk_size, embed // blk_size)
    heads = heads.transpose(1, 3, 0, 2, 4).reshape((y_size * blk_size, 2) + heads.shape[2:3] + heads.shape[4:])
    heads = lax.all_to_all(heads, ("y", "blk"), 0, 0, tiled=True)
    heads = jnp.sum(heads, axis=0)
    heads = heads / weight_total
    return (loss_sum / weight_total, heads[0], heads[1])


def solution(mesh):
    dp_size = mesh.shape["dp"]
    blk_size = mesh.shape["blk"]
    lanes = mesh.devices.reshape(dp_size // 8, 4, 2, blk_size)
    fine = Mesh(lanes, ("y", "x", "core", "blk"))
    rows = ("y", "x", "core")
    placed = (P(rows, "blk", None), P(rows, "blk", None), P(rows, "blk"), P(rows, "blk"), P(), P())
    return jax.shard_map(
        per_device,
        mesh=fine,
        in_specs=placed,
        out_specs=(P(), P(rows, "blk"), P(rows, "blk")),
        check_vma=False,
    )
```

```python
import jax
import jax.numpy as jnp
from jax import lax
from jax.sharding import Mesh, PartitionSpec as P

EPS = 1e-06
LOGIT_SCALE = 50.0


def embed_rows(features, weight):
    projected_raw = jnp.dot(features, weight, preferred_element_type=jnp.float32)
    radius = jnp.sqrt(jnp.sum(projected_raw * projected_raw, axis=1, keepdims=True) + EPS)
    unit_vec = projected_raw / radius
    return (unit_vec, unit_vec.astype(jnp.bfloat16), radius)


def similarity(queries, key_rows):
    return LOGIT_SCALE * lax.dot_general(
        queries, key_rows, (((1,), (1,)), ((), ())), preferred_element_type=jnp.float32
    )


def coefficient(scores, matches, weights, totals):
    probability = jnp.exp(scores - LOGIT_SCALE) / totals[:, None]
    return (weights[:, None] * (probability - matches.astype(jnp.float32))).astype(jnp.bfloat16)


def back_norm(unit_vec, radius, gradient):
    projected = jnp.sum(unit_vec * gradient, axis=1, keepdims=True)
    return ((gradient - unit_vec * projected) / radius).astype(jnp.bfloat16)


def gathered_sum(value):
    axes = ("y", "x", "core", "blk")
    count = 1
    for axis in axes:
        count *= lax.axis_size(axis)
    spread = jnp.broadcast_to(value.reshape(1, 1), (count, 1))
    return jnp.sum(lax.all_to_all(spread, axes, 0, 0, tiled=True))


def per_device(prod_feat, prec_feat, matched, row_weight, proj_prod, proj_prec):
    feat_prod = prod_feat[0]
    feat_prec = prec_feat[0]
    targets = matched[0]
    weights = row_weight[0]
    unit_prod, unit16_prod, radius_prod = embed_rows(feat_prod, proj_prod)
    feat_prec_all = lax.all_gather(feat_prec, "blk", axis=0, tiled=True)
    unit_prec, unit16_prec, radius_prec = embed_rows(feat_prec_all, proj_prec)
    scores = similarity(unit16_prod, unit16_prec)
    columns = lax.iota(jnp.int32, unit16_prec.shape[0])
    matches = targets[:, None] == columns[None, :]
    totals = jnp.sum(jnp.exp(scores - LOGIT_SCALE), axis=1)
    positive = jnp.sum(jnp.where(matches, scores, 0.0), axis=1)
    losses = LOGIT_SCALE + jnp.log(totals) - positive
    loss_local = jnp.sum(weights * losses)
    weight_local = jnp.sum(weights)
    loss_sum = gathered_sum(loss_local)
    weight_total = gathered_sum(weight_local)
    coeffs = coefficient(scores, matches, weights, totals)
    grad_unit_prod = LOGIT_SCALE * jnp.dot(coeffs, unit16_prec, preferred_element_type=jnp.float32)
    grad_prec_part = LOGIT_SCALE * lax.dot_general(
        coeffs, unit16_prod, (((0,), (0,)), ((), ())), preferred_element_type=jnp.float32
    )
    dir_prod = back_norm(unit_prod, radius_prod, grad_unit_prod)
    dir_prec = back_norm(unit_prec, radius_prec, grad_prec_part)
    head_prod = lax.dot_general(
        feat_prod, dir_prod, (((0,), (0,)), ((), ())), preferred_element_type=jnp.float32
    )
    head_prec = lax.dot_general(
        feat_prec_all, dir_prec, (((0,), (0,)), ((), ())), preferred_element_type=jnp.float32
    )
    heads = jnp.stack([head_prod, head_prec])
    feat, embed = head_prod.shape
    y_size = lax.axis_size("y")
    x_size = lax.axis_size("x")
    core_size = lax.axis_size("core")
    heads = heads.reshape(2, y_size, x_size, core_size, feat // (y_size * x_size * core_size), embed)
    heads = lax.psum_scatter(heads, "core", scatter_dimension=3, tiled=False)
    heads = lax.psum_scatter(heads, "x", scatter_dimension=2, tiled=False)
    blk_size = lax.axis_size("blk")
    heads = heads.reshape(2, y_size, feat // (y_size * x_size * core_size), blk_size, embed // blk_size)
    heads = heads.transpose(1, 3, 0, 2, 4).reshape((y_size * blk_size, 2) + heads.shape[2:3] + heads.shape[4:])
    heads = lax.all_to_all(heads, ("y", "blk"), 0, 0, tiled=True)
    heads = jnp.sum(heads, axis=0)
    heads = heads / weight_total
    return (loss_sum / weight_total, heads[0], heads[1])


def solution(mesh):
    dp_size = mesh.shape["dp"]
    blk_size = mesh.shape["blk"]
    lanes = mesh.devices.reshape(dp_size // 8, 4, 2, blk_size)
    fine = Mesh(lanes, ("y", "x", "core", "blk"))
    rows = ("y", "x", "core")
    placed = (P(rows, "blk", None), P(rows, "blk", None), P(rows, "blk"), P(rows, "blk"), P(), P())
    return jax.shard_map(
        per_device,
        mesh=fine,
        in_specs=placed,
        out_specs=(P(), P(rows, "blk"), P(rows, "blk")),
        check_vma=False,
    )
```

```python
import jax
import jax.numpy as jnp
from jax import lax
from jax.sharding import Mesh, PartitionSpec as P

EPS = 1e-06
LOGIT_SCALE = 50.0


def embed_rows(features, weight):
    projected_raw = jnp.dot(features, weight, preferred_element_type=jnp.float32)
    radius = jnp.sqrt(jnp.sum(projected_raw * projected_raw, axis=1, keepdims=True) + EPS)
    unit_vec = projected_raw / radius
    return (unit_vec, unit_vec.astype(jnp.bfloat16), radius)


def similarity(queries, key_rows):
    return LOGIT_SCALE * lax.dot_general(
        queries, key_rows, (((1,), (1,)), ((), ())), preferred_element_type=jnp.float32
    )


def coefficient(scores, matches, weights, totals):
    probability = jnp.exp(scores - LOGIT_SCALE) / totals[:, None]
    return (weights[:, None] * (probability - matches.astype(jnp.float32))).astype(jnp.bfloat16)


def back_norm(unit_vec, radius, gradient):
    projected = jnp.sum(unit_vec * gradient, axis=1, keepdims=True)
    return ((gradient - unit_vec * projected) / radius).astype(jnp.bfloat16)


def gathered_sum(value):
    axes = ("y", "x", "core", "blk")
    count = 1
    for axis in axes:
        count *= lax.axis_size(axis)
    spread = jnp.broadcast_to(value.reshape(1, 1), (count, 1))
    return jnp.sum(lax.all_to_all(spread, axes, 0, 0, tiled=True))


def per_device(prod_feat, prec_feat, matched, row_weight, proj_prod, proj_prec):
    feat_prod = prod_feat[0]
    feat_prec = prec_feat[0]
    targets = matched[0]
    weights = row_weight[0]
    unit_prod, unit16_prod, radius_prod = embed_rows(feat_prod, proj_prod)
    feat_prec_all = lax.all_gather(feat_prec, "blk", axis=0, tiled=True)
    unit_prec, unit16_prec, radius_prec = embed_rows(feat_prec_all, proj_prec)
    scores = similarity(unit16_prod, unit16_prec)
    columns = lax.iota(jnp.int32, unit16_prec.shape[0])
    matches = targets[:, None] == columns[None, :]
    totals = jnp.sum(jnp.exp(scores - LOGIT_SCALE), axis=1)
    positive = jnp.sum(jnp.where(matches, scores, 0.0), axis=1)
    losses = LOGIT_SCALE + jnp.log(totals) - positive
    loss_local = jnp.sum(weights * losses)
    weight_local = jnp.sum(weights)
    loss_sum = gathered_sum(loss_local)
    weight_total = gathered_sum(weight_local)
    coeffs = coefficient(scores, matches, weights, totals)
    grad_unit_prod = LOGIT_SCALE * jnp.dot(coeffs, unit16_prec, preferred_element_type=jnp.float32)
    grad_prec_part = LOGIT_SCALE * lax.dot_general(
        coeffs, unit16_prod, (((0,), (0,)), ((), ())), preferred_element_type=jnp.float32
    )
    dir_prod = back_norm(unit_prod, radius_prod, grad_unit_prod)
    dir_prec = back_norm(unit_prec, radius_prec, grad_prec_part)
    head_prod = lax.dot_general(
        feat_prod, dir_prod, (((0,), (0,)), ((), ())), preferred_element_type=jnp.float32
    )
    head_prec = lax.dot_general(
        feat_prec_all, dir_prec, (((0,), (0,)), ((), ())), preferred_element_type=jnp.float32
    )
    heads = jnp.stack([head_prod, head_prec])
    feat, embed = head_prod.shape
    y_size = lax.axis_size("y")
    x_size = lax.axis_size("x")
    core_size = lax.axis_size("core")
    heads = heads.reshape(2, y_size, x_size, core_size, feat // (y_size * x_size * core_size), embed)
    heads = lax.psum_scatter(heads, "core", scatter_dimension=3, tiled=False)
    blk_size = lax.axis_size("blk")
    block_rows = feat // (y_size * x_size * core_size)
    heads = heads.reshape(2, y_size, x_size, block_rows, blk_size, embed // blk_size)
    heads = heads.transpose(1, 2, 4, 0, 3, 5)
    heads = heads.reshape((y_size * x_size * blk_size, 2, block_rows, embed // blk_size))
    heads = lax.all_to_all(heads, ("y", "x", "blk"), 0, 0, tiled=True)
    heads = jnp.sum(heads, axis=0)
    heads = heads / weight_total
    return (loss_sum / weight_total, heads[0], heads[1])


def solution(mesh):
    dp_size = mesh.shape["dp"]
    blk_size = mesh.shape["blk"]
    lanes = mesh.devices.reshape(dp_size // 8, 4, 2, blk_size)
    fine = Mesh(lanes, ("y", "x", "core", "blk"))
    rows = ("y", "x", "core")
    placed = (P(rows, "blk", None), P(rows, "blk", None), P(rows, "blk"), P(rows, "blk"), P(), P())
    return jax.shard_map(
        per_device,
        mesh=fine,
        in_specs=placed,
        out_specs=(P(), P(rows, "blk"), P(rows, "blk")),
        check_vma=False,
    )
```

```python
import jax
import jax.numpy as jnp
from jax import lax
from jax.sharding import Mesh, PartitionSpec as P

EPS = 1e-06
LOGIT_SCALE = 50.0


def embed_rows(features, weight):
    projected_raw = jnp.dot(features, weight, preferred_element_type=jnp.float32)
    radius = jnp.sqrt(jnp.sum(projected_raw * projected_raw, axis=1, keepdims=True) + EPS)
    unit_vec = projected_raw / radius
    return (unit_vec, unit_vec.astype(jnp.bfloat16), radius)


def similarity(queries, key_rows):
    return LOGIT_SCALE * lax.dot_general(
        queries, key_rows, (((1,), (1,)), ((), ())), preferred_element_type=jnp.float32
    )


def coefficient(scores, matches, weights, totals):
    probability = jnp.exp(scores - LOGIT_SCALE) / totals[:, None]
    return (weights[:, None] * (probability - matches.astype(jnp.float32))).astype(jnp.bfloat16)


def back_norm(unit_vec, radius, gradient):
    projected = jnp.sum(unit_vec * gradient, axis=1, keepdims=True)
    return ((gradient - unit_vec * projected) / radius).astype(jnp.bfloat16)


def gathered_sum(value):
    axes = ("y", "x", "core", "blk")
    count = 1
    for axis in axes:
        count *= lax.axis_size(axis)
    spread = jnp.broadcast_to(value.reshape(1, 1), (count, 1))
    return jnp.sum(lax.all_to_all(spread, axes, 0, 0, tiled=True))


def per_device(prod_feat, prec_feat, matched, row_weight, proj_prod, proj_prec):
    feat_prod = prod_feat[0]
    feat_prec = prec_feat[0]
    targets = matched[0]
    weights = row_weight[0]
    row_count = feat_prec.shape[0]
    blk_size = lax.axis_size("blk")
    blk_pos = lax.axis_index("blk")
    from_next = lax.ppermute(feat_prec, "blk", [(i, (i - 1) % blk_size) for i in range(blk_size)])
    from_prev = lax.ppermute(feat_prec, "blk", [(i, (i + 1) % blk_size) for i in range(blk_size)])
    half = row_count // 2
    low_half = lax.ppermute(from_prev[:half], "blk", [(i, (i + 1) % blk_size) for i in range(blk_size)])
    high_half = lax.ppermute(from_next[half:], "blk", [(i, (i - 1) % blk_size) for i in range(blk_size)])
    opposite = jnp.concatenate([low_half, high_half], axis=0)
    blocks = [feat_prec, from_next, from_prev, opposite]
    sources = [blk_pos, (blk_pos + 1) % blk_size, (blk_pos - 1) % blk_size, (blk_pos + 2) % blk_size]
    unit_prod, unit16_prod, radius_prod = embed_rows(feat_prod, proj_prod)
    embedded = [embed_rows(block, proj_prec) for block in blocks]
    scores = [similarity(unit16_prod, unit16) for (_, unit16, _) in embedded]
    local_columns = lax.iota(jnp.int32, row_count)
    matches = [targets[:, None] == (source * row_count + local_columns)[None, :] for source in sources]
    totals = sum(jnp.sum(jnp.exp(block_scores - LOGIT_SCALE), axis=1) for block_scores in scores)
    positive = sum(
        jnp.sum(jnp.where(block_matches, block_scores, 0.0), axis=1)
        for block_matches, block_scores in zip(matches, scores)
    )
    losses = LOGIT_SCALE + jnp.log(totals) - positive
    loss_local = jnp.sum(weights * losses)
    weight_local = jnp.sum(weights)
    loss_sum = gathered_sum(loss_local)
    weight_total = gathered_sum(weight_local)
    grad_unit_prod = 0.0
    head_prec = 0.0
    for block, (unit_prec, unit16_prec, radius_prec), block_scores, block_matches in zip(
        blocks, embedded, scores, matches
    ):
        coeffs = coefficient(block_scores, block_matches, weights, totals)
        grad_unit_prod = grad_unit_prod + jnp.dot(coeffs, unit16_prec, preferred_element_type=jnp.float32)
        grad_prec_part = LOGIT_SCALE * lax.dot_general(
            coeffs, unit16_prod, (((0,), (0,)), ((), ())), preferred_element_type=jnp.float32
        )
        dir_prec = back_norm(unit_prec, radius_prec, grad_prec_part)
        head_prec = head_prec + lax.dot_general(
            block, dir_prec, (((0,), (0,)), ((), ())), preferred_element_type=jnp.float32
        )
    dir_prod = back_norm(unit_prod, radius_prod, LOGIT_SCALE * grad_unit_prod)
    head_prod = lax.dot_general(
        feat_prod, dir_prod, (((0,), (0,)), ((), ())), preferred_element_type=jnp.float32
    )
    heads = jnp.stack([head_prod, head_prec])
    feat, embed = head_prod.shape
    y_size = lax.axis_size("y")
    x_size = lax.axis_size("x")
    core_size = lax.axis_size("core")
    heads = heads.reshape(2, y_size, x_size, core_size, feat // (y_size * x_size * core_size), embed)
    heads = lax.psum_scatter(heads, "core", scatter_dimension=3, tiled=False)
    heads = lax.psum_scatter(heads, "x", scatter_dimension=2, tiled=False)
    blk_size = lax.axis_size("blk")
    heads = heads.reshape(2, y_size, feat // (y_size * x_size * core_size), blk_size, embed // blk_size)
    heads = heads.transpose(1, 3, 0, 2, 4).reshape((y_size * blk_size, 2) + heads.shape[2:3] + heads.shape[4:])
    heads = lax.all_to_all(heads, ("y", "blk"), 0, 0, tiled=True)
    heads = jnp.sum(heads, axis=0)
    heads = heads / weight_total
    return (loss_sum / weight_total, heads[0], heads[1])


def solution(mesh):
    dp_size = mesh.shape["dp"]
    blk_size = mesh.shape["blk"]
    lanes = mesh.devices.reshape(dp_size // 8, 4, 2, blk_size)
    fine = Mesh(lanes, ("y", "x", "core", "blk"))
    rows = ("y", "x", "core")
    placed = (P(rows, "blk", None), P(rows, "blk", None), P(rows, "blk"), P(rows, "blk"), P(), P())
    return jax.shard_map(
        per_device,
        mesh=fine,
        in_specs=placed,
        out_specs=(P(), P(rows, "blk"), P(rows, "blk")),
        check_vma=False,
    )
```

```python
import jax
import jax.numpy as jnp
from jax import lax
from jax.sharding import Mesh, PartitionSpec as P

EPS = 1e-06
LOGIT_SCALE = 50.0


def embed_rows(features, weight):
    projected_raw = jnp.dot(features, weight, preferred_element_type=jnp.float32)
    radius = jnp.sqrt(jnp.sum(projected_raw * projected_raw, axis=1, keepdims=True) + EPS)
    unit_vec = projected_raw / radius
    return (unit_vec, unit_vec.astype(jnp.bfloat16), radius)


def similarity(queries, key_rows):
    return LOGIT_SCALE * lax.dot_general(
        queries, key_rows, (((1,), (1,)), ((), ())), preferred_element_type=jnp.float32
    )


def coefficient(scores, matches, weights, totals):
    probability = jnp.exp(scores - LOGIT_SCALE) / totals[:, None]
    return (weights[:, None] * (probability - matches.astype(jnp.float32))).astype(jnp.bfloat16)


def back_norm(unit_vec, radius, gradient):
    projected = jnp.sum(unit_vec * gradient, axis=1, keepdims=True)
    return ((gradient - unit_vec * projected) / radius).astype(jnp.bfloat16)


def gathered_sum(values):
    axes = ("y", "x", "core", "blk")
    count = 1
    for axis in axes:
        count *= lax.axis_size(axis)
    spread = jnp.broadcast_to(values.reshape((1,) + values.shape), (count,) + values.shape)
    return jnp.sum(lax.all_to_all(spread, axes, 0, 0, tiled=True), axis=0)


def per_device(prod_feat, prec_feat, matched, row_weight, proj_prod, proj_prec):
    feat_prod = prod_feat[0]
    feat_prec = prec_feat[0]
    targets = matched[0]
    weights = row_weight[0]
    row_count = feat_prec.shape[0]
    blk_size = lax.axis_size("blk")
    blk_pos = lax.axis_index("blk")
    from_next = lax.ppermute(feat_prec, "blk", [(i, (i - 1) % blk_size) for i in range(blk_size)])
    from_prev = lax.ppermute(feat_prec, "blk", [(i, (i + 1) % blk_size) for i in range(blk_size)])
    half = row_count // 2
    low_half = lax.ppermute(from_prev[:half], "blk", [(i, (i + 1) % blk_size) for i in range(blk_size)])
    high_half = lax.ppermute(from_next[half:], "blk", [(i, (i - 1) % blk_size) for i in range(blk_size)])
    opposite = jnp.concatenate([low_half, high_half], axis=0)
    blocks = [feat_prec, from_next, from_prev, opposite]
    sources = [blk_pos, (blk_pos + 1) % blk_size, (blk_pos - 1) % blk_size, (blk_pos + 2) % blk_size]
    unit_prod, unit16_prod, radius_prod = embed_rows(feat_prod, proj_prod)
    embedded = [embed_rows(block, proj_prec) for block in blocks]
    scores = [similarity(unit16_prod, unit16) for (_, unit16, _) in embedded]
    local_columns = lax.iota(jnp.int32, row_count)
    matches = [targets[:, None] == (source * row_count + local_columns)[None, :] for source in sources]
    totals = sum(jnp.sum(jnp.exp(block_scores - LOGIT_SCALE), axis=1) for block_scores in scores)
    positive = sum(
        jnp.sum(jnp.where(block_matches, block_scores, 0.0), axis=1)
        for block_matches, block_scores in zip(matches, scores)
    )
    losses = LOGIT_SCALE + jnp.log(totals) - positive
    loss_local = jnp.sum(weights * losses)
    weight_local = jnp.sum(weights)
    loss_sum, weight_total = gathered_sum(jnp.stack([loss_local, weight_local]))
    grad_unit_prod = 0.0
    head_prec = 0.0
    for block, (unit_prec, unit16_prec, radius_prec), block_scores, block_matches in zip(
        blocks, embedded, scores, matches
    ):
        coeffs = coefficient(block_scores, block_matches, weights, totals)
        grad_unit_prod = grad_unit_prod + jnp.dot(coeffs, unit16_prec, preferred_element_type=jnp.float32)
        grad_prec_part = LOGIT_SCALE * lax.dot_general(
            coeffs, unit16_prod, (((0,), (0,)), ((), ())), preferred_element_type=jnp.float32
        )
        dir_prec = back_norm(unit_prec, radius_prec, grad_prec_part)
        head_prec = head_prec + lax.dot_general(
            block, dir_prec, (((0,), (0,)), ((), ())), preferred_element_type=jnp.float32
        )
    dir_prod = back_norm(unit_prod, radius_prod, LOGIT_SCALE * grad_unit_prod)
    head_prod = lax.dot_general(
        feat_prod, dir_prod, (((0,), (0,)), ((), ())), preferred_element_type=jnp.float32
    )
    heads = jnp.stack([head_prod, head_prec])
    feat, embed = head_prod.shape
    y_size = lax.axis_size("y")
    x_size = lax.axis_size("x")
    core_size = lax.axis_size("core")
    heads = heads.reshape(2, y_size, x_size, core_size, feat // (y_size * x_size * core_size), embed)
    heads = lax.psum_scatter(heads, "core", scatter_dimension=3, tiled=False)
    heads = lax.psum_scatter(heads, "x", scatter_dimension=2, tiled=False)
    blk_size = lax.axis_size("blk")
    heads = heads.reshape(2, y_size, feat // (y_size * x_size * core_size), blk_size, embed // blk_size)
    heads = heads.transpose(1, 3, 0, 2, 4).reshape((y_size * blk_size, 2) + heads.shape[2:3] + heads.shape[4:])
    heads = lax.all_to_all(heads, ("y", "blk"), 0, 0, tiled=True)
    heads = jnp.sum(heads, axis=0)
    heads = heads / weight_total
    return (loss_sum / weight_total, heads[0], heads[1])


def solution(mesh):
    dp_size = mesh.shape["dp"]
    blk_size = mesh.shape["blk"]
    lanes = mesh.devices.reshape(dp_size // 8, 4, 2, blk_size)
    fine = Mesh(lanes, ("y", "x", "core", "blk"))
    rows = ("y", "x", "core")
    placed = (P(rows, "blk", None), P(rows, "blk", None), P(rows, "blk"), P(rows, "blk"), P(), P())
    return jax.shard_map(
        per_device,
        mesh=fine,
        in_specs=placed,
        out_specs=(P(), P(rows, "blk"), P(rows, "blk")),
        check_vma=False,
    )
```

```python
import jax
import jax.numpy as jnp
from jax import lax
from jax.sharding import Mesh, PartitionSpec as P

EPS = 1e-06
LOGIT_SCALE = 50.0


def embed_rows(features, weight):
    projected_raw = jnp.dot(features, weight, preferred_element_type=jnp.float32)
    radius = jnp.sqrt(jnp.sum(projected_raw * projected_raw, axis=1, keepdims=True) + EPS)
    unit_vec = projected_raw / radius
    return (unit_vec, unit_vec.astype(jnp.bfloat16), radius)


def similarity(queries, key_rows):
    return LOGIT_SCALE * lax.dot_general(
        queries, key_rows, (((1,), (1,)), ((), ())), preferred_element_type=jnp.float32
    )


def coefficient(scores, matches, weights, totals):
    probability = jnp.exp(scores - LOGIT_SCALE) / totals[:, None]
    return (weights[:, None] * (probability - matches.astype(jnp.float32))).astype(jnp.bfloat16)


def back_norm(unit_vec, radius, gradient):
    projected = jnp.sum(unit_vec * gradient, axis=1, keepdims=True)
    return ((gradient - unit_vec * projected) / radius).astype(jnp.bfloat16)


def gathered_sum(values):
    axes = ("y", "x", "core", "blk")
    count = 1
    for axis in axes:
        count *= lax.axis_size(axis)
    spread = jnp.broadcast_to(values.reshape((1,) + values.shape), (count,) + values.shape)
    return jnp.sum(lax.all_to_all(spread, axes, 0, 0, tiled=True), axis=0)


def reduce_head(head):
    feat, embed = head.shape
    y_size = lax.axis_size("y")
    x_size = lax.axis_size("x")
    core_size = lax.axis_size("core")
    blk_size = lax.axis_size("blk")
    block_rows = feat // (y_size * x_size * core_size)
    head = head.reshape(y_size, x_size, core_size, block_rows, embed)
    head = lax.psum_scatter(head, "core", scatter_dimension=2, tiled=False)
    head = lax.psum_scatter(head, "x", scatter_dimension=1, tiled=False)
    head = head.reshape(y_size, block_rows, blk_size, embed // blk_size).transpose(0, 2, 1, 3)
    head = head.reshape(y_size * blk_size, block_rows, embed // blk_size)
    head = lax.all_to_all(head, ("y", "blk"), 0, 0, tiled=True)
    return jnp.sum(head, axis=0)


def per_device(prod_feat, prec_feat, matched, row_weight, proj_prod, proj_prec):
    feat_prod = prod_feat[0]
    feat_prec = prec_feat[0]
    targets = matched[0]
    weights = row_weight[0]
    row_count = feat_prec.shape[0]
    blk_size = lax.axis_size("blk")
    blk_pos = lax.axis_index("blk")
    from_next = lax.ppermute(feat_prec, "blk", [(i, (i - 1) % blk_size) for i in range(blk_size)])
    from_prev = lax.ppermute(feat_prec, "blk", [(i, (i + 1) % blk_size) for i in range(blk_size)])
    half = row_count // 2
    low_half = lax.ppermute(from_prev[:half], "blk", [(i, (i + 1) % blk_size) for i in range(blk_size)])
    high_half = lax.ppermute(from_next[half:], "blk", [(i, (i - 1) % blk_size) for i in range(blk_size)])
    opposite = jnp.concatenate([low_half, high_half], axis=0)
    blocks = [feat_prec, from_next, from_prev, opposite]
    sources = [blk_pos, (blk_pos + 1) % blk_size, (blk_pos - 1) % blk_size, (blk_pos + 2) % blk_size]
    unit_prod, unit16_prod, radius_prod = embed_rows(feat_prod, proj_prod)
    embedded = [embed_rows(block, proj_prec) for block in blocks]
    scores = [similarity(unit16_prod, unit16) for (_, unit16, _) in embedded]
    local_columns = lax.iota(jnp.int32, row_count)
    matches = [targets[:, None] == (source * row_count + local_columns)[None, :] for source in sources]
    totals = sum(jnp.sum(jnp.exp(block_scores - LOGIT_SCALE), axis=1) for block_scores in scores)
    positive = sum(
        jnp.sum(jnp.where(block_matches, block_scores, 0.0), axis=1)
        for block_matches, block_scores in zip(matches, scores)
    )
    losses = LOGIT_SCALE + jnp.log(totals) - positive
    loss_local = jnp.sum(weights * losses)
    weight_local = jnp.sum(weights)
    loss_sum, weight_total = gathered_sum(jnp.stack([loss_local, weight_local]))
    grad_unit_prod = 0.0
    for (unit_prec, unit16_prec, radius_prec), block_scores, block_matches in zip(embedded, scores, matches):
        coeffs = coefficient(block_scores, block_matches, weights, totals)
        grad_unit_prod = grad_unit_prod + jnp.dot(coeffs, unit16_prec, preferred_element_type=jnp.float32)
    dir_prod = back_norm(unit_prod, radius_prod, LOGIT_SCALE * grad_unit_prod)
    head_prod = lax.dot_general(
        feat_prod, dir_prod, (((0,), (0,)), ((), ())), preferred_element_type=jnp.float32
    )
    summed_prod = reduce_head(head_prod)
    head_prec = 0.0
    for block, (unit_prec, unit16_prec, radius_prec), block_scores, block_matches in zip(
        blocks, embedded, scores, matches
    ):
        coeffs = coefficient(block_scores, block_matches, weights, totals)
        grad_prec_part = LOGIT_SCALE * lax.dot_general(
            coeffs, unit16_prod, (((0,), (0,)), ((), ())), preferred_element_type=jnp.float32
        )
        dir_prec = back_norm(unit_prec, radius_prec, grad_prec_part)
        head_prec = head_prec + lax.dot_general(
            block, dir_prec, (((0,), (0,)), ((), ())), preferred_element_type=jnp.float32
        )
    summed_prec = reduce_head(head_prec)
    heads = jnp.stack([summed_prod, summed_prec])
    heads = heads / weight_total
    return (loss_sum / weight_total, heads[0], heads[1])


def solution(mesh):
    dp_size = mesh.shape["dp"]
    blk_size = mesh.shape["blk"]
    lanes = mesh.devices.reshape(dp_size // 8, 4, 2, blk_size)
    fine = Mesh(lanes, ("y", "x", "core", "blk"))
    rows = ("y", "x", "core")
    placed = (P(rows, "blk", None), P(rows, "blk", None), P(rows, "blk"), P(rows, "blk"), P(), P())
    return jax.shard_map(
        per_device,
        mesh=fine,
        in_specs=placed,
        out_specs=(P(), P(rows, "blk"), P(rows, "blk")),
        check_vma=False,
    )
```

```python
import jax
import jax.numpy as jnp
from jax import lax
from jax.sharding import Mesh, PartitionSpec as P

EPS = 1e-06
LOGIT_SCALE = 50.0


def embed_rows(features, weight):
    projected_raw = jnp.dot(features, weight, preferred_element_type=jnp.float32)
    radius = jnp.sqrt(jnp.sum(projected_raw * projected_raw, axis=1, keepdims=True) + EPS)
    unit_vec = projected_raw / radius
    return (unit_vec, unit_vec.astype(jnp.bfloat16), radius)


def similarity(queries, key_rows):
    return LOGIT_SCALE * lax.dot_general(
        queries, key_rows, (((1,), (1,)), ((), ())), preferred_element_type=jnp.float32
    )


def coefficient(scores, matches, weights, totals):
    probability = jnp.exp(scores - LOGIT_SCALE) / totals[:, None]
    return (weights[:, None] * (probability - matches.astype(jnp.float32))).astype(jnp.bfloat16)


def back_norm(unit_vec, radius, gradient):
    projected = jnp.sum(unit_vec * gradient, axis=1, keepdims=True)
    return ((gradient - unit_vec * projected) / radius).astype(jnp.bfloat16)


def gathered_sum(values):
    axes = ("y", "x", "core", "blk")
    count = 1
    for axis in axes:
        count *= lax.axis_size(axis)
    spread = jnp.broadcast_to(values.reshape((1,) + values.shape), (count,) + values.shape)
    return jnp.sum(lax.all_to_all(spread, axes, 0, 0, tiled=True), axis=0)


def per_device(prod_feat, prec_feat, matched, row_weight, proj_prod, proj_prec):
    feat_prod = prod_feat[0]
    feat_prec = prec_feat[0]
    targets = matched[0]
    weights = row_weight[0]
    row_count = feat_prec.shape[0]
    blk_size = lax.axis_size("blk")
    blk_pos = lax.axis_index("blk")
    from_next = lax.ppermute(feat_prec, "blk", [(i, (i - 1) % blk_size) for i in range(blk_size)])
    from_prev = lax.ppermute(feat_prec, "blk", [(i, (i + 1) % blk_size) for i in range(blk_size)])
    half = row_count // 2
    low_half = lax.ppermute(from_prev[:half], "blk", [(i, (i + 1) % blk_size) for i in range(blk_size)])
    high_half = lax.ppermute(from_next[half:], "blk", [(i, (i - 1) % blk_size) for i in range(blk_size)])
    opposite = jnp.concatenate([low_half, high_half], axis=0)
    near = jnp.concatenate([feat_prec, from_next, from_prev], axis=0)
    blocks = [near, opposite]
    near_order = jnp.stack([blk_pos, (blk_pos + 1) % blk_size, (blk_pos - 1) % blk_size])
    sources = [near_order, ((blk_pos + 2) % blk_size).reshape(1)]
    unit_prod, unit16_prod, radius_prod = embed_rows(feat_prod, proj_prod)
    embedded = [embed_rows(block, proj_prec) for block in blocks]
    scores = [similarity(unit16_prod, unit16) for (_, unit16, _) in embedded]
    local_columns = lax.iota(jnp.int32, row_count)
    matches = [
        targets[:, None] == (source[:, None] * row_count + local_columns[None, :]).reshape(1, -1)
        for source in sources
    ]
    totals = sum(jnp.sum(jnp.exp(block_scores - LOGIT_SCALE), axis=1) for block_scores in scores)
    positive = sum(
        jnp.sum(jnp.where(block_matches, block_scores, 0.0), axis=1)
        for block_matches, block_scores in zip(matches, scores)
    )
    losses = LOGIT_SCALE + jnp.log(totals) - positive
    loss_local = jnp.sum(weights * losses)
    weight_local = jnp.sum(weights)
    loss_sum, weight_total = gathered_sum(jnp.stack([loss_local, weight_local]))
    grad_unit_prod = 0.0
    head_prec = 0.0
    for block, (unit_prec, unit16_prec, radius_prec), block_scores, block_matches in zip(
        blocks, embedded, scores, matches
    ):
        coeffs = coefficient(block_scores, block_matches, weights, totals)
        grad_unit_prod = grad_unit_prod + jnp.dot(coeffs, unit16_prec, preferred_element_type=jnp.float32)
        grad_prec_part = LOGIT_SCALE * lax.dot_general(
            coeffs, unit16_prod, (((0,), (0,)), ((), ())), preferred_element_type=jnp.float32
        )
        dir_prec = back_norm(unit_prec, radius_prec, grad_prec_part)
        head_prec = head_prec + lax.dot_general(
            block, dir_prec, (((0,), (0,)), ((), ())), preferred_element_type=jnp.float32
        )
    dir_prod = back_norm(unit_prod, radius_prod, LOGIT_SCALE * grad_unit_prod)
    head_prod = lax.dot_general(
        feat_prod, dir_prod, (((0,), (0,)), ((), ())), preferred_element_type=jnp.float32
    )
    heads = jnp.stack([head_prod, head_prec])
    feat, embed = head_prod.shape
    y_size = lax.axis_size("y")
    x_size = lax.axis_size("x")
    core_size = lax.axis_size("core")
    heads = heads.reshape(2, y_size, x_size, core_size, feat // (y_size * x_size * core_size), embed)
    heads = lax.psum_scatter(heads, "core", scatter_dimension=3, tiled=False)
    heads = lax.psum_scatter(heads, "x", scatter_dimension=2, tiled=False)
    blk_size = lax.axis_size("blk")
    heads = heads.reshape(2, y_size, feat // (y_size * x_size * core_size), blk_size, embed // blk_size)
    heads = heads.transpose(1, 3, 0, 2, 4).reshape((y_size * blk_size, 2) + heads.shape[2:3] + heads.shape[4:])
    heads = lax.all_to_all(heads, ("y", "blk"), 0, 0, tiled=True)
    heads = jnp.sum(heads, axis=0)
    heads = heads / weight_total
    return (loss_sum / weight_total, heads[0], heads[1])


def solution(mesh):
    dp_size = mesh.shape["dp"]
    blk_size = mesh.shape["blk"]
    lanes = mesh.devices.reshape(dp_size // 8, 4, 2, blk_size)
    fine = Mesh(lanes, ("y", "x", "core", "blk"))
    rows = ("y", "x", "core")
    placed = (P(rows, "blk", None), P(rows, "blk", None), P(rows, "blk"), P(rows, "blk"), P(), P())
    return jax.shard_map(
        per_device,
        mesh=fine,
        in_specs=placed,
        out_specs=(P(), P(rows, "blk"), P(rows, "blk")),
        check_vma=False,
    )
```

```python
import jax
import jax.numpy as jnp
from jax import lax
from jax.sharding import Mesh, PartitionSpec as P

EPS = 1e-06
LOGIT_SCALE = 50.0


def embed_rows(features, weight):
    projected_raw = jnp.dot(features, weight, preferred_element_type=jnp.float32)
    radius = jnp.sqrt(jnp.sum(projected_raw * projected_raw, axis=1, keepdims=True) + EPS)
    unit_vec = projected_raw / radius
    return (unit_vec, unit_vec.astype(jnp.bfloat16), radius)


def similarity(queries, key_rows):
    return LOGIT_SCALE * lax.dot_general(
        queries, key_rows, (((1,), (1,)), ((), ())), preferred_element_type=jnp.float32
    )


def coefficient(scores, matches, weights, totals):
    probability = jnp.exp(scores - LOGIT_SCALE) / totals[:, None]
    return (weights[:, None] * (probability - matches.astype(jnp.float32))).astype(jnp.bfloat16)


def back_norm(unit_vec, radius, gradient):
    projected = jnp.sum(unit_vec * gradient, axis=1, keepdims=True)
    return ((gradient - unit_vec * projected) / radius).astype(jnp.bfloat16)


def gathered_sum(values):
    axes = ("y", "x", "core", "blk")
    count = 1
    for axis in axes:
        count *= lax.axis_size(axis)
    spread = jnp.broadcast_to(values.reshape((1,) + values.shape), (count,) + values.shape)
    return jnp.sum(lax.all_to_all(spread, axes, 0, 0, tiled=True), axis=0)


def per_device(prod_feat, prec_feat, matched, row_weight, proj_prod, proj_prec):
    feat_prod = prod_feat[0]
    feat_prec = prec_feat[0]
    targets = matched[0]
    weights = row_weight[0]
    row_count = feat_prec.shape[0]
    blk_size = lax.axis_size("blk")
    blk_pos = lax.axis_index("blk")
    from_next = lax.ppermute(feat_prec, "blk", [(i, (i - 1) % blk_size) for i in range(blk_size)])
    from_prev = lax.ppermute(feat_prec, "blk", [(i, (i + 1) % blk_size) for i in range(blk_size)])
    half = row_count // 2
    low_half = lax.ppermute(from_prev[:half], "blk", [(i, (i + 1) % blk_size) for i in range(blk_size)])
    high_half = lax.ppermute(from_next[half:], "blk", [(i, (i - 1) % blk_size) for i in range(blk_size)])
    opposite = jnp.concatenate([low_half, high_half], axis=0)
    near = jnp.concatenate([feat_prec, from_next, from_prev], axis=0)
    blocks = [near, opposite]
    near_order = jnp.stack([blk_pos, (blk_pos + 1) % blk_size, (blk_pos - 1) % blk_size])
    sources = [near_order, ((blk_pos + 2) % blk_size).reshape(1)]
    unit_prod, unit16_prod, radius_prod = embed_rows(feat_prod, proj_prod)
    embedded = [embed_rows(block, proj_prec) for block in blocks]
    scores = [similarity(unit16_prod, unit16) for (_, unit16, _) in embedded]
    local_columns = lax.iota(jnp.int32, row_count)
    matches = [
        targets[:, None] == (source[:, None] * row_count + local_columns[None, :]).reshape(1, -1)
        for source in sources
    ]
    totals = sum(jnp.sum(jnp.exp(block_scores - LOGIT_SCALE), axis=1) for block_scores in scores)
    positive = sum(
        jnp.sum(jnp.where(block_matches, block_scores, 0.0), axis=1)
        for block_matches, block_scores in zip(matches, scores)
    )
    losses = LOGIT_SCALE + jnp.log(totals) - positive
    loss_local = jnp.sum(weights * losses)
    weight_local = jnp.sum(weights)
    loss_sum, weight_total = gathered_sum(jnp.stack([loss_local, weight_local]))
    grad_unit_prod = 0.0
    head_prec = 0.0
    for block, (unit_prec, unit16_prec, radius_prec), block_scores, block_matches in zip(
        blocks, embedded, scores, matches
    ):
        coeffs = coefficient(block_scores, block_matches, weights, totals)
        grad_unit_prod = grad_unit_prod + jnp.dot(coeffs, unit16_prec, preferred_element_type=jnp.float32)
        grad_prec_part = LOGIT_SCALE * lax.dot_general(
            coeffs, unit16_prod, (((0,), (0,)), ((), ())), preferred_element_type=jnp.float32
        )
        dir_prec = back_norm(unit_prec, radius_prec, grad_prec_part)
        head_prec = head_prec + lax.dot_general(
            block, dir_prec, (((0,), (0,)), ((), ())), preferred_element_type=jnp.float32
        )
    dir_prod = back_norm(unit_prod, radius_prod, LOGIT_SCALE * grad_unit_prod)
    head_prod = lax.dot_general(
        feat_prod, dir_prod, (((0,), (0,)), ((), ())), preferred_element_type=jnp.float32
    )
    heads = jnp.stack([head_prod, head_prec])
    feat, embed = head_prod.shape
    y_size = lax.axis_size("y")
    x_size = lax.axis_size("x")
    core_size = lax.axis_size("core")
    block_rows = feat // (y_size * x_size * core_size)
    heads = heads.reshape(2, y_size, x_size, core_size, block_rows, embed)
    heads = lax.psum_scatter(heads, "core", scatter_dimension=3, tiled=False)
    blk_size = lax.axis_size("blk")
    cols = embed // blk_size
    heads = heads.reshape(2, y_size, x_size, block_rows, blk_size, cols)
    prod_part = heads[0].transpose(1, 0, 2, 3, 4)
    prod_part = jnp.sum(lax.all_to_all(prod_part, "x", 0, 0, tiled=True), axis=0)
    prod_part = prod_part.transpose(0, 2, 1, 3).reshape(y_size * blk_size, block_rows, cols)
    prod_part = jnp.sum(lax.all_to_all(prod_part, ("y", "blk"), 0, 0, tiled=True), axis=0)
    prec_part = lax.psum_scatter(heads[1], "blk", scatter_dimension=3, tiled=False)
    prec_part = prec_part.reshape(y_size * x_size, block_rows, cols)
    prec_part = jnp.sum(lax.all_to_all(prec_part, ("y", "x"), 0, 0, tiled=True), axis=0)
    heads = jnp.stack([prod_part, prec_part])
    heads = heads / weight_total
    return (loss_sum / weight_total, heads[0], heads[1])


def solution(mesh):
    dp_size = mesh.shape["dp"]
    blk_size = mesh.shape["blk"]
    lanes = mesh.devices.reshape(dp_size // 8, 4, 2, blk_size)
    fine = Mesh(lanes, ("y", "x", "core", "blk"))
    rows = ("y", "x", "core")
    placed = (P(rows, "blk", None), P(rows, "blk", None), P(rows, "blk"), P(rows, "blk"), P(), P())
    return jax.shard_map(
        per_device,
        mesh=fine,
        in_specs=placed,
        out_specs=(P(), P(rows, "blk"), P(rows, "blk")),
        check_vma=False,
    )
```

```python
import jax
import jax.numpy as jnp
from jax import lax
from jax.sharding import Mesh, PartitionSpec as P

EPS = 1e-06
LOGIT_SCALE = 50.0


def embed_rows(features, weight):
    projected_raw = jnp.dot(features, weight, preferred_element_type=jnp.float32)
    radius = jnp.sqrt(jnp.sum(projected_raw * projected_raw, axis=1, keepdims=True) + EPS)
    unit_vec = projected_raw / radius
    return (unit_vec, unit_vec.astype(jnp.bfloat16), radius)


def similarity(queries, key_rows):
    return LOGIT_SCALE * lax.dot_general(
        queries, key_rows, (((1,), (1,)), ((), ())), preferred_element_type=jnp.float32
    )


def coefficient(scores, matches, weights, totals):
    probability = jnp.exp(scores - LOGIT_SCALE) / totals[:, None]
    return (weights[:, None] * (probability - matches.astype(jnp.float32))).astype(jnp.bfloat16)


def back_norm(unit_vec, radius, gradient):
    projected = jnp.sum(unit_vec * gradient, axis=1, keepdims=True)
    return ((gradient - unit_vec * projected) / radius).astype(jnp.bfloat16)


def gathered_sum(values):
    axes = ("y", "x", "core", "blk")
    count = 1
    for axis in axes:
        count *= lax.axis_size(axis)
    spread = jnp.broadcast_to(values.reshape((1,) + values.shape), (count,) + values.shape)
    return jnp.sum(lax.all_to_all(spread, axes, 0, 0, tiled=True), axis=0)


def per_device(prod_feat, prec_feat, matched, row_weight, proj_prod, proj_prec):
    feat_prod = prod_feat[0]
    feat_prec = prec_feat[0]
    targets = matched[0]
    weights = row_weight[0]
    row_count = feat_prec.shape[0]
    blk_size = lax.axis_size("blk")
    blk_pos = lax.axis_index("blk")
    from_next = lax.ppermute(feat_prec, "blk", [(i, (i - 1) % blk_size) for i in range(blk_size)])
    from_prev = lax.ppermute(feat_prec, "blk", [(i, (i + 1) % blk_size) for i in range(blk_size)])
    half = row_count // 2
    low_half = lax.ppermute(from_prev[:half], "blk", [(i, (i + 1) % blk_size) for i in range(blk_size)])
    high_half = lax.ppermute(from_next[half:], "blk", [(i, (i - 1) % blk_size) for i in range(blk_size)])
    opposite = jnp.concatenate([low_half, high_half], axis=0)
    near = jnp.concatenate([from_next, from_prev], axis=0)
    blocks = [feat_prec, near, opposite]
    near_order = jnp.stack([(blk_pos + 1) % blk_size, (blk_pos - 1) % blk_size])
    sources = [blk_pos.reshape(1), near_order, ((blk_pos + 2) % blk_size).reshape(1)]
    unit_prod, unit16_prod, radius_prod = embed_rows(feat_prod, proj_prod)
    embedded = [embed_rows(block, proj_prec) for block in blocks]
    scores = [similarity(unit16_prod, unit16) for (_, unit16, _) in embedded]
    local_columns = lax.iota(jnp.int32, row_count)
    matches = [
        targets[:, None] == (source[:, None] * row_count + local_columns[None, :]).reshape(1, -1)
        for source in sources
    ]
    totals = sum(jnp.sum(jnp.exp(block_scores - LOGIT_SCALE), axis=1) for block_scores in scores)
    positive = sum(
        jnp.sum(jnp.where(block_matches, block_scores, 0.0), axis=1)
        for block_matches, block_scores in zip(matches, scores)
    )
    losses = LOGIT_SCALE + jnp.log(totals) - positive
    loss_local = jnp.sum(weights * losses)
    weight_local = jnp.sum(weights)
    loss_sum, weight_total = gathered_sum(jnp.stack([loss_local, weight_local]))
    grad_unit_prod = 0.0
    head_prec = 0.0
    for block, (unit_prec, unit16_prec, radius_prec), block_scores, block_matches in zip(
        blocks, embedded, scores, matches
    ):
        coeffs = coefficient(block_scores, block_matches, weights, totals)
        grad_unit_prod = grad_unit_prod + jnp.dot(coeffs, unit16_prec, preferred_element_type=jnp.float32)
        grad_prec_part = LOGIT_SCALE * lax.dot_general(
            coeffs, unit16_prod, (((0,), (0,)), ((), ())), preferred_element_type=jnp.float32
        )
        dir_prec = back_norm(unit_prec, radius_prec, grad_prec_part)
        head_prec = head_prec + lax.dot_general(
            block, dir_prec, (((0,), (0,)), ((), ())), preferred_element_type=jnp.float32
        )
    dir_prod = back_norm(unit_prod, radius_prod, LOGIT_SCALE * grad_unit_prod)
    head_prod = lax.dot_general(
        feat_prod, dir_prod, (((0,), (0,)), ((), ())), preferred_element_type=jnp.float32
    )
    heads = jnp.stack([head_prod, head_prec])
    feat, embed = head_prod.shape
    y_size = lax.axis_size("y")
    x_size = lax.axis_size("x")
    core_size = lax.axis_size("core")
    heads = heads.reshape(2, y_size, x_size, core_size, feat // (y_size * x_size * core_size), embed)
    heads = lax.psum_scatter(heads, "core", scatter_dimension=3, tiled=False)
    heads = lax.psum_scatter(heads, "x", scatter_dimension=2, tiled=False)
    blk_size = lax.axis_size("blk")
    heads = heads.reshape(2, y_size, feat // (y_size * x_size * core_size), blk_size, embed // blk_size)
    heads = heads.transpose(1, 3, 0, 2, 4).reshape((y_size * blk_size, 2) + heads.shape[2:3] + heads.shape[4:])
    heads = lax.all_to_all(heads, ("y", "blk"), 0, 0, tiled=True)
    heads = jnp.sum(heads, axis=0)
    heads = heads / weight_total
    return (loss_sum / weight_total, heads[0], heads[1])


def solution(mesh):
    dp_size = mesh.shape["dp"]
    blk_size = mesh.shape["blk"]
    lanes = mesh.devices.reshape(dp_size // 8, 4, 2, blk_size)
    fine = Mesh(lanes, ("y", "x", "core", "blk"))
    rows = ("y", "x", "core")
    placed = (P(rows, "blk", None), P(rows, "blk", None), P(rows, "blk"), P(rows, "blk"), P(), P())
    return jax.shard_map(
        per_device,
        mesh=fine,
        in_specs=placed,
        out_specs=(P(), P(rows, "blk"), P(rows, "blk")),
        check_vma=False,
    )
```

```python
import jax
import jax.numpy as jnp
from jax import lax
from jax.sharding import Mesh, PartitionSpec as P

EPS = 1e-06
LOGIT_SCALE = 50.0


def embed_rows(features, weight):
    projected_raw = jnp.dot(features, weight, preferred_element_type=jnp.float32)
    radius = jnp.sqrt(jnp.sum(projected_raw * projected_raw, axis=1, keepdims=True) + EPS)
    unit_vec = projected_raw / radius
    return (unit_vec, unit_vec.astype(jnp.bfloat16), radius)


def similarity(queries, key_rows):
    return LOGIT_SCALE * lax.dot_general(
        queries, key_rows, (((1,), (1,)), ((), ())), preferred_element_type=jnp.float32
    )


def coefficient(scores, matches, weights, totals):
    probability = jnp.exp(scores - LOGIT_SCALE) / totals[:, None]
    return (weights[:, None] * (probability - matches.astype(jnp.float32))).astype(jnp.bfloat16)


def back_norm(unit_vec, radius, gradient):
    projected = jnp.sum(unit_vec * gradient, axis=1, keepdims=True)
    return ((gradient - unit_vec * projected) / radius).astype(jnp.bfloat16)


def gathered_sum(values):
    axes = ("y", "x", "core", "blk")
    count = 1
    for axis in axes:
        count *= lax.axis_size(axis)
    spread = jnp.broadcast_to(values.reshape((1,) + values.shape), (count,) + values.shape)
    return jnp.sum(lax.all_to_all(spread, axes, 0, 0, tiled=True), axis=0)


def per_device(prod_feat, prec_feat, matched, row_weight, proj_prod, proj_prec):
    feat_prod = prod_feat[0]
    feat_prec = prec_feat[0]
    targets = matched[0]
    weights = row_weight[0]
    row_count = feat_prec.shape[0]
    blk_size = lax.axis_size("blk")
    blk_pos = lax.axis_index("blk")
    from_next = lax.ppermute(feat_prec, "blk", [(i, (i - 1) % blk_size) for i in range(blk_size)])
    from_prev = lax.ppermute(feat_prec, "blk", [(i, (i + 1) % blk_size) for i in range(blk_size)])
    half = row_count // 2
    low_half = lax.ppermute(from_prev[:half], "blk", [(i, (i + 1) % blk_size) for i in range(blk_size)])
    high_half = lax.ppermute(from_next[half:], "blk", [(i, (i - 1) % blk_size) for i in range(blk_size)])
    opposite = jnp.concatenate([low_half, high_half], axis=0)
    near = jnp.concatenate([feat_prec, from_next, from_prev], axis=0)
    blocks = [near, opposite]
    near_order = jnp.stack([blk_pos, (blk_pos + 1) % blk_size, (blk_pos - 1) % blk_size])
    sources = [near_order, ((blk_pos + 2) % blk_size).reshape(1)]
    unit_prod, unit16_prod, radius_prod = embed_rows(feat_prod, proj_prod)
    embedded = [embed_rows(block, proj_prec) for block in blocks]
    scores = [similarity(unit16_prod, unit16) for (_, unit16, _) in embedded]
    local_columns = lax.iota(jnp.int32, row_count)
    matches = [
        targets[:, None] == (source[:, None] * row_count + local_columns[None, :]).reshape(1, -1)
        for source in sources
    ]
    totals = sum(jnp.sum(jnp.exp(block_scores - LOGIT_SCALE), axis=1) for block_scores in scores)
    positive = sum(
        jnp.sum(jnp.where(block_matches, block_scores, 0.0), axis=1)
        for block_matches, block_scores in zip(matches, scores)
    )
    losses = LOGIT_SCALE + jnp.log(totals) - positive
    loss_local = jnp.sum(weights * losses)
    weight_local = jnp.sum(weights)
    loss_sum, weight_total = gathered_sum(jnp.stack([loss_local, weight_local]))
    grad_unit_prod = 0.0
    head_prec = 0.0
    for block, (unit_prec, unit16_prec, radius_prec), block_scores, block_matches in zip(
        blocks, embedded, scores, matches
    ):
        coeffs = coefficient(block_scores, block_matches, weights, totals)
        grad_unit_prod = grad_unit_prod + jnp.dot(coeffs, unit16_prec, preferred_element_type=jnp.float32)
        grad_prec_part = LOGIT_SCALE * lax.dot_general(
            coeffs, unit16_prod, (((0,), (0,)), ((), ())), preferred_element_type=jnp.float32
        )
        dir_prec = back_norm(unit_prec, radius_prec, grad_prec_part)
        head_prec = head_prec + lax.dot_general(
            block, dir_prec, (((0,), (0,)), ((), ())), preferred_element_type=jnp.float32
        )
    dir_prod = back_norm(unit_prod, radius_prod, LOGIT_SCALE * grad_unit_prod)
    head_prod = lax.dot_general(
        feat_prod, dir_prod, (((0,), (0,)), ((), ())), preferred_element_type=jnp.float32
    )
    heads = jnp.stack([head_prod, head_prec])
    feat, embed = head_prod.shape
    y_size = lax.axis_size("y")
    x_size = lax.axis_size("x")
    core_size = lax.axis_size("core")
    heads = heads.reshape(2, y_size, x_size, core_size, feat // (y_size * x_size * core_size), embed)
    heads = lax.psum_scatter(heads, "core", scatter_dimension=3, tiled=False)
    blk_size = lax.axis_size("blk")
    block_rows = feat // (y_size * x_size * core_size)
    cols = embed // blk_size
    heads = heads.reshape(2, y_size, x_size, block_rows, blk_size, cols).transpose(2, 4, 0, 1, 3, 5)
    heads = heads.reshape((x_size * blk_size, 2, y_size, block_rows, cols))
    heads = jnp.sum(lax.all_to_all(heads, ("x", "blk"), 0, 0, tiled=True), axis=0)
    heads = heads.transpose(1, 0, 2, 3)
    heads = jnp.sum(lax.all_to_all(heads, "y", 0, 0, tiled=True), axis=0)
    heads = heads / weight_total
    return (loss_sum / weight_total, heads[0], heads[1])


def solution(mesh):
    dp_size = mesh.shape["dp"]
    blk_size = mesh.shape["blk"]
    lanes = mesh.devices.reshape(dp_size // 8, 4, 2, blk_size)
    fine = Mesh(lanes, ("y", "x", "core", "blk"))
    rows = ("y", "x", "core")
    placed = (P(rows, "blk", None), P(rows, "blk", None), P(rows, "blk"), P(rows, "blk"), P(), P())
    return jax.shard_map(
        per_device,
        mesh=fine,
        in_specs=placed,
        out_specs=(P(), P(rows, "blk"), P(rows, "blk")),
        check_vma=False,
    )
```

```python
import jax
import jax.numpy as jnp
from jax import lax
from jax.sharding import Mesh, PartitionSpec as P

EPS = 1e-06
LOGIT_SCALE = 50.0


def embed_rows(features, weight):
    projected_raw = jnp.dot(features, weight, preferred_element_type=jnp.float32)
    radius = jnp.sqrt(jnp.sum(projected_raw * projected_raw, axis=1, keepdims=True) + EPS)
    unit_vec = projected_raw / radius
    return (unit_vec, unit_vec.astype(jnp.bfloat16), radius)


def similarity(queries, key_rows):
    return LOGIT_SCALE * lax.dot_general(
        queries, key_rows, (((1,), (1,)), ((), ())), preferred_element_type=jnp.float32
    )


def coefficient(scores, matches, weights, totals):
    probability = jnp.exp(scores - LOGIT_SCALE) / totals[:, None]
    return (weights[:, None] * (probability - matches.astype(jnp.float32))).astype(jnp.bfloat16)


def back_norm(unit_vec, radius, gradient):
    projected = jnp.sum(unit_vec * gradient, axis=1, keepdims=True)
    return ((gradient - unit_vec * projected) / radius).astype(jnp.bfloat16)


def gathered_sum(values):
    axes = ("y", "x", "core", "blk")
    count = 1
    for axis in axes:
        count *= lax.axis_size(axis)
    spread = jnp.broadcast_to(values.reshape((1,) + values.shape), (count,) + values.shape)
    return jnp.sum(lax.all_to_all(spread, axes, 0, 0, tiled=True), axis=0)


def per_device(prod_feat, prec_feat, matched, row_weight, proj_prod, proj_prec):
    feat_prod = prod_feat[0]
    feat_prec = prec_feat[0]
    targets = matched[0]
    weights = row_weight[0]
    row_count = feat_prec.shape[0]
    blk_size = lax.axis_size("blk")
    blk_pos = lax.axis_index("blk")
    from_next = lax.ppermute(feat_prec, "blk", [(i, (i - 1) % blk_size) for i in range(blk_size)])
    from_prev = lax.ppermute(feat_prec, "blk", [(i, (i + 1) % blk_size) for i in range(blk_size)])
    half = row_count // 2
    low_half = lax.ppermute(from_prev[:half], "blk", [(i, (i + 1) % blk_size) for i in range(blk_size)])
    high_half = lax.ppermute(from_next[half:], "blk", [(i, (i - 1) % blk_size) for i in range(blk_size)])
    opposite = jnp.concatenate([low_half, high_half], axis=0)
    near = jnp.concatenate([feat_prec, from_next, from_prev], axis=0)
    blocks = [near, opposite]
    near_order = jnp.stack([blk_pos, (blk_pos + 1) % blk_size, (blk_pos - 1) % blk_size])
    sources = [near_order, ((blk_pos + 2) % blk_size).reshape(1)]
    unit_prod, unit16_prod, radius_prod = embed_rows(feat_prod, proj_prod)
    embedded = [embed_rows(block, proj_prec) for block in blocks]
    scores = [similarity(unit16_prod, unit16) for (_, unit16, _) in embedded]
    local_columns = lax.iota(jnp.int32, row_count)
    matches = [
        targets[:, None] == (source[:, None] * row_count + local_columns[None, :]).reshape(1, -1)
        for source in sources
    ]
    totals = sum(jnp.sum(jnp.exp(block_scores - LOGIT_SCALE), axis=1) for block_scores in scores)
    positive = sum(
        jnp.sum(jnp.where(block_matches, block_scores, 0.0), axis=1)
        for block_matches, block_scores in zip(matches, scores)
    )
    losses = LOGIT_SCALE + jnp.log(totals) - positive
    loss_local = jnp.sum(weights * losses)
    weight_local = jnp.sum(weights)
    loss_sum, weight_total = gathered_sum(jnp.stack([loss_local, weight_local]))
    grad_unit_prod = 0.0
    head_prec = 0.0
    for block, (unit_prec, unit16_prec, radius_prec), block_scores, block_matches in zip(
        blocks, embedded, scores, matches
    ):
        coeffs = lax.optimization_barrier(coefficient(block_scores, block_matches, weights, totals))
        grad_unit_prod = grad_unit_prod + jnp.dot(coeffs, unit16_prec, preferred_element_type=jnp.float32)
        grad_prec_part = LOGIT_SCALE * lax.dot_general(
            coeffs, unit16_prod, (((0,), (0,)), ((), ())), preferred_element_type=jnp.float32
        )
        dir_prec = back_norm(unit_prec, radius_prec, grad_prec_part)
        head_prec = head_prec + lax.dot_general(
            block, dir_prec, (((0,), (0,)), ((), ())), preferred_element_type=jnp.float32
        )
    dir_prod = back_norm(unit_prod, radius_prod, LOGIT_SCALE * grad_unit_prod)
    head_prod = lax.dot_general(
        feat_prod, dir_prod, (((0,), (0,)), ((), ())), preferred_element_type=jnp.float32
    )
    heads = jnp.stack([head_prod, head_prec])
    feat, embed = head_prod.shape
    y_size = lax.axis_size("y")
    x_size = lax.axis_size("x")
    core_size = lax.axis_size("core")
    heads = heads.reshape(2, y_size, x_size, core_size, feat // (y_size * x_size * core_size), embed)
    heads = lax.psum_scatter(heads, "core", scatter_dimension=3, tiled=False)
    heads = lax.psum_scatter(heads, "x", scatter_dimension=2, tiled=False)
    blk_size = lax.axis_size("blk")
    heads = heads.reshape(2, y_size, feat // (y_size * x_size * core_size), blk_size, embed // blk_size)
    heads = heads.transpose(1, 3, 0, 2, 4).reshape((y_size * blk_size, 2) + heads.shape[2:3] + heads.shape[4:])
    heads = lax.all_to_all(heads, ("y", "blk"), 0, 0, tiled=True)
    heads = jnp.sum(heads, axis=0)
    heads = heads / weight_total
    return (loss_sum / weight_total, heads[0], heads[1])


def solution(mesh):
    dp_size = mesh.shape["dp"]
    blk_size = mesh.shape["blk"]
    lanes = mesh.devices.reshape(dp_size // 8, 4, 2, blk_size)
    fine = Mesh(lanes, ("y", "x", "core", "blk"))
    rows = ("y", "x", "core")
    placed = (P(rows, "blk", None), P(rows, "blk", None), P(rows, "blk"), P(rows, "blk"), P(), P())
    return jax.shard_map(
        per_device,
        mesh=fine,
        in_specs=placed,
        out_specs=(P(), P(rows, "blk"), P(rows, "blk")),
        check_vma=False,
    )
```

```python
import jax
import jax.numpy as jnp
from jax import lax
from jax.sharding import Mesh, PartitionSpec as P

EPS = 1e-06
LOGIT_SCALE = 50.0


def embed_rows(features, weight):
    projected_raw = jnp.dot(features, weight, preferred_element_type=jnp.float32)
    radius = jnp.sqrt(jnp.sum(projected_raw * projected_raw, axis=1, keepdims=True) + EPS)
    unit_vec = projected_raw / radius
    return (unit_vec, unit_vec.astype(jnp.bfloat16), radius)


def similarity(queries, key_rows):
    return LOGIT_SCALE * lax.dot_general(
        queries, key_rows, (((1,), (1,)), ((), ())), preferred_element_type=jnp.float32
    )


def coefficient(scores, matches, weights, totals):
    probability = jnp.exp(scores - LOGIT_SCALE) / totals[:, None]
    return (weights[:, None] * (probability - matches.astype(jnp.float32))).astype(jnp.bfloat16)


def back_norm(unit_vec, radius, gradient):
    projected = jnp.sum(unit_vec * gradient, axis=1, keepdims=True)
    return ((gradient - unit_vec * projected) / radius).astype(jnp.bfloat16)


def gathered_sum(values):
    axes = ("y", "x", "core", "blk")
    count = 1
    for axis in axes:
        count *= lax.axis_size(axis)
    spread = jnp.broadcast_to(values.reshape((1,) + values.shape), (count,) + values.shape)
    return jnp.sum(lax.all_to_all(spread, axes, 0, 0, tiled=True), axis=0)


def per_device(prod_feat, prec_feat, matched, row_weight, proj_prod, proj_prec):
    feat_prod = prod_feat[0]
    feat_prec = prec_feat[0]
    targets = matched[0]
    weights = row_weight[0]
    row_count = feat_prec.shape[0]
    blk_size = lax.axis_size("blk")
    blk_pos = lax.axis_index("blk")
    from_next = lax.ppermute(feat_prec, "blk", [(i, (i - 1) % blk_size) for i in range(blk_size)])
    from_prev = lax.ppermute(feat_prec, "blk", [(i, (i + 1) % blk_size) for i in range(blk_size)])
    half = row_count // 2
    low_half = lax.ppermute(from_prev[:half], "blk", [(i, (i + 1) % blk_size) for i in range(blk_size)])
    high_half = lax.ppermute(from_next[half:], "blk", [(i, (i - 1) % blk_size) for i in range(blk_size)])
    opposite = jnp.concatenate([low_half, high_half], axis=0)
    near = jnp.concatenate([feat_prec, from_next, from_prev], axis=0)
    blocks = [near, opposite]
    near_order = jnp.stack([blk_pos, (blk_pos + 1) % blk_size, (blk_pos - 1) % blk_size])
    sources = [near_order, ((blk_pos + 2) % blk_size).reshape(1)]
    unit_prod, unit16_prod, radius_prod = embed_rows(feat_prod, proj_prod)
    embedded = [embed_rows(block, proj_prec) for block in blocks]
    scores = [similarity(unit16_prod, unit16) for (_, unit16, _) in embedded]
    local_columns = lax.iota(jnp.int32, row_count)
    matches = [
        targets[:, None] == (source[:, None] * row_count + local_columns[None, :]).reshape(1, -1)
        for source in sources
    ]
    totals = sum(jnp.sum(jnp.exp(block_scores - LOGIT_SCALE), axis=1) for block_scores in scores)
    positive = sum(
        jnp.sum(jnp.where(block_matches, block_scores, 0.0), axis=1)
        for block_matches, block_scores in zip(matches, scores)
    )
    losses = LOGIT_SCALE + jnp.log(totals) - positive
    loss_local = jnp.sum(weights * losses)
    weight_local = jnp.sum(weights)
    loss_sum, weight_total = gathered_sum(jnp.stack([loss_local, weight_local]))
    grad_unit_prod = 0.0
    head_prec = 0.0
    for block, (unit_prec, unit16_prec, radius_prec), block_scores, block_matches in zip(
        blocks, embedded, scores, matches
    ):
        coeffs = coefficient(block_scores, block_matches, weights, totals)
        grad_unit_prod = grad_unit_prod + jnp.dot(coeffs, unit16_prec, preferred_element_type=jnp.float32)
        grad_prec_part = LOGIT_SCALE * lax.dot_general(
            coeffs, unit16_prod, (((0,), (0,)), ((), ())), preferred_element_type=jnp.float32
        )
        dir_prec = back_norm(unit_prec, radius_prec, grad_prec_part)
        head_prec = head_prec + lax.dot_general(
            dir_prec, block, (((0,), (0,)), ((), ())), preferred_element_type=jnp.float32
        )
    dir_prod = back_norm(unit_prod, radius_prod, LOGIT_SCALE * grad_unit_prod)
    head_prod = lax.dot_general(
        feat_prod, dir_prod, (((0,), (0,)), ((), ())), preferred_element_type=jnp.float32
    )
    heads = jnp.stack([head_prod, head_prec.T])
    feat, embed = head_prod.shape
    y_size = lax.axis_size("y")
    x_size = lax.axis_size("x")
    core_size = lax.axis_size("core")
    heads = heads.reshape(2, y_size, x_size, core_size, feat // (y_size * x_size * core_size), embed)
    heads = lax.psum_scatter(heads, "core", scatter_dimension=3, tiled=False)
    heads = lax.psum_scatter(heads, "x", scatter_dimension=2, tiled=False)
    blk_size = lax.axis_size("blk")
    heads = heads.reshape(2, y_size, feat // (y_size * x_size * core_size), blk_size, embed // blk_size)
    heads = heads.transpose(1, 3, 0, 2, 4).reshape((y_size * blk_size, 2) + heads.shape[2:3] + heads.shape[4:])
    heads = lax.all_to_all(heads, ("y", "blk"), 0, 0, tiled=True)
    heads = jnp.sum(heads, axis=0)
    heads = heads / weight_total
    return (loss_sum / weight_total, heads[0], heads[1])


def solution(mesh):
    dp_size = mesh.shape["dp"]
    blk_size = mesh.shape["blk"]
    lanes = mesh.devices.reshape(dp_size // 8, 4, 2, blk_size)
    fine = Mesh(lanes, ("y", "x", "core", "blk"))
    rows = ("y", "x", "core")
    placed = (P(rows, "blk", None), P(rows, "blk", None), P(rows, "blk"), P(rows, "blk"), P(), P())
    return jax.shard_map(
        per_device,
        mesh=fine,
        in_specs=placed,
        out_specs=(P(), P(rows, "blk"), P(rows, "blk")),
        check_vma=False,
    )
```

```python
import jax
import jax.numpy as jnp
from jax import lax
from jax.sharding import Mesh, PartitionSpec as P

EPS = 1e-06
LOGIT_SCALE = 50.0


def embed_rows(features, weight):
    projected_raw = jnp.dot(features, weight, preferred_element_type=jnp.float32)
    radius = jnp.sqrt(jnp.sum(projected_raw * projected_raw, axis=1, keepdims=True) + EPS)
    unit_vec = projected_raw / radius
    return (unit_vec, unit_vec.astype(jnp.bfloat16), radius)


def similarity(queries, key_rows):
    return LOGIT_SCALE * lax.dot_general(
        queries, key_rows, (((1,), (1,)), ((), ())), preferred_element_type=jnp.float32
    )


def coefficient(scores, matches, weights, totals):
    probability = jnp.exp(scores - LOGIT_SCALE) / totals[:, None]
    return (weights[:, None] * (probability - matches.astype(jnp.float32))).astype(jnp.bfloat16)


def back_norm(unit_vec, radius, gradient):
    projected = jnp.sum(unit_vec * gradient, axis=1, keepdims=True)
    return ((gradient - unit_vec * projected) / radius).astype(jnp.bfloat16)


def gathered_sum(values):
    axes = ("y", "x", "core", "blk")
    count = 1
    for axis in axes:
        count *= lax.axis_size(axis)
    spread = jnp.broadcast_to(values.reshape((1,) + values.shape), (count,) + values.shape)
    return jnp.sum(lax.all_to_all(spread, axes, 0, 0, tiled=True), axis=0)


def per_device(prod_feat, prec_feat, matched, row_weight, proj_prod, proj_prec):
    feat_prod = prod_feat[0]
    feat_prec = prec_feat[0]
    targets = matched[0]
    weights = row_weight[0]
    row_count = feat_prec.shape[0]
    blk_size = lax.axis_size("blk")
    blk_pos = lax.axis_index("blk")
    from_next = lax.ppermute(feat_prec, "blk", [(i, (i - 1) % blk_size) for i in range(blk_size)])
    from_prev = lax.ppermute(feat_prec, "blk", [(i, (i + 1) % blk_size) for i in range(blk_size)])
    half = row_count // 2
    low_half = lax.ppermute(from_prev[:half], "blk", [(i, (i + 1) % blk_size) for i in range(blk_size)])
    high_half = lax.ppermute(from_next[half:], "blk", [(i, (i - 1) % blk_size) for i in range(blk_size)])
    opposite = jnp.concatenate([low_half, high_half], axis=0)
    near = jnp.concatenate([feat_prec, from_next, from_prev], axis=0)
    blocks = [near, opposite]
    near_order = jnp.stack([blk_pos, (blk_pos + 1) % blk_size, (blk_pos - 1) % blk_size])
    sources = [near_order, ((blk_pos + 2) % blk_size).reshape(1)]
    unit_prod, unit16_prod, radius_prod = embed_rows(feat_prod, proj_prod)
    embedded = [embed_rows(block, proj_prec) for block in blocks]
    scores = [similarity(unit16_prod, unit16) for (_, unit16, _) in embedded]
    local_columns = lax.iota(jnp.int32, row_count)
    matches = [
        targets[:, None] == (source[:, None] * row_count + local_columns[None, :]).reshape(1, -1)
        for source in sources
    ]
    totals = sum(jnp.sum(jnp.exp(block_scores - LOGIT_SCALE), axis=1) for block_scores in scores)
    positive = sum(
        jnp.sum(jnp.where(block_matches, block_scores, 0.0), axis=1)
        for block_matches, block_scores in zip(matches, scores)
    )
    losses = LOGIT_SCALE + jnp.log(totals) - positive
    loss_local = jnp.sum(weights * losses)
    weight_local = jnp.sum(weights)
    loss_sum, weight_total = gathered_sum(jnp.stack([loss_local, weight_local]))
    grad_unit_prod = 0.0
    dirs_prec = []
    for (unit_prec, unit16_prec, radius_prec), block_scores, block_matches in zip(embedded, scores, matches):
        coeffs = coefficient(block_scores, block_matches, weights, totals)
        grad_unit_prod = grad_unit_prod + jnp.dot(coeffs, unit16_prec, preferred_element_type=jnp.float32)
        grad_prec_part = LOGIT_SCALE * lax.dot_general(
            coeffs, unit16_prod, (((0,), (0,)), ((), ())), preferred_element_type=jnp.float32
        )
        dirs_prec.append(back_norm(unit_prec, radius_prec, grad_prec_part))
    dir_prod = back_norm(unit_prod, radius_prod, LOGIT_SCALE * grad_unit_prod)
    heads = lax.dot_general(
        jnp.stack([feat_prod, opposite]),
        jnp.stack([dir_prod, dirs_prec[1]]),
        (((1,), (1,)), ((0,), (0,))),
        preferred_element_type=jnp.float32,
    )
    near_head = lax.dot_general(
        dirs_prec[0], near, (((0,), (0,)), ((), ())), preferred_element_type=jnp.float32
    )
    heads = heads + jnp.stack([jnp.zeros_like(near_head.T), near_head.T])
    head_prod = heads[0]
    feat, embed = head_prod.shape
    y_size = lax.axis_size("y")
    x_size = lax.axis_size("x")
    core_size = lax.axis_size("core")
    heads = heads.reshape(2, y_size, x_size, core_size, feat // (y_size * x_size * core_size), embed)
    heads = lax.psum_scatter(heads, "core", scatter_dimension=3, tiled=False)
    heads = lax.psum_scatter(heads, "x", scatter_dimension=2, tiled=False)
    blk_size = lax.axis_size("blk")
    heads = heads.reshape(2, y_size, feat // (y_size * x_size * core_size), blk_size, embed // blk_size)
    heads = heads.transpose(1, 3, 0, 2, 4).reshape((y_size * blk_size, 2) + heads.shape[2:3] + heads.shape[4:])
    heads = lax.all_to_all(heads, ("y", "blk"), 0, 0, tiled=True)
    heads = jnp.sum(heads, axis=0)
    heads = heads / weight_total
    return (loss_sum / weight_total, heads[0], heads[1])


def solution(mesh):
    dp_size = mesh.shape["dp"]
    blk_size = mesh.shape["blk"]
    lanes = mesh.devices.reshape(dp_size // 8, 4, 2, blk_size)
    fine = Mesh(lanes, ("y", "x", "core", "blk"))
    rows = ("y", "x", "core")
    placed = (P(rows, "blk", None), P(rows, "blk", None), P(rows, "blk"), P(rows, "blk"), P(), P())
    return jax.shard_map(
        per_device,
        mesh=fine,
        in_specs=placed,
        out_specs=(P(), P(rows, "blk"), P(rows, "blk")),
        check_vma=False,
    )
```
